128 devices in a mesh: ctx: 16 (over y, x_lo, core), head: 8 (over x_hi, z).
Axes of the slice: x: 4 (x_hi: 2, x_lo: 2; x = x_hi * 2 + x_lo), y: 4, z: 4, core: 2. Of those that a mesh axis runs over, the one named last changes fastest.
Arguments:
- queries: bfloat16 [4096, 5120], P('ctx', 'head'), may hold values from -6 to 6
- keys: bfloat16 [4096, 5120], P('ctx', 'head'), may hold values from -6 to 6
- values: bfloat16 [4096, 5120], P('ctx', 'head'), may hold values from -16 to 16
- out_weight: bfloat16 [5120, 5120], P('head'), may hold values from -0.078125 to 0.078125
- cotangent: bfloat16 [4096, 5120], P('ctx', 'head'), may hold values from -16 to 16
- contacts: int32 [32, 32], replicated, may hold values 0 or 1
- chains: int32 [32], replicated, may hold values from 0 to 3, never falling along the last dimension, each value on 1 to 16 neighbouring positions
Outputs:
- mixed: bfloat16 [4096, 5120], P('ctx', 'head')
- query_grad: bfloat16 [4096, 5120], P('ctx', 'head')
- key_grad: bfloat16 [4096, 5120], P('ctx', 'head')
- value_grad: bfloat16 [4096, 5120], P('ctx', 'head')
The draws below stay inside these ranges and needn't reach their ends.
Inputs may be any that keep to these rules, and one draw needn't show every extreme that they name: `chains`: chain numbers never fall along the blocks; each chain has 1 to 16 blocks, one exactly 16.
All inputs are finite; a program needn't handle non-finite values.
Results may differ from the reference program's by a relative error of at most 0.02.
Values may be sent and summed in bfloat16 or wider, within the bound.
No kernel may reach another device: no remote copies, remote signals or barrier semaphores. Data moves between devices by JAX's collectives and lax.ppermute only.
A program may use at most 192 MiB of HBM per device.

```python
import math
import jax
import jax.numpy as jnp
import numpy as np
from jax import lax

HEAD_SIZE = 128
HEADS = 40
D_MODEL = 5120
BLOCK = 128
CHAINS = 4
ROWS_DEV = 256
LENGTH = 4096
NBLOCKS = 32
N_CTX = 16


def drawn_pair(key):
    first = jax.random.fold_in(key, 11)
    second = jax.random.fold_in(key, 12)
    query_part = jnp.clip(jax.random.normal(first, (LENGTH, D_MODEL), jnp.float32), -5.0, 5.0)
    key_part = jnp.clip(jax.random.normal(second, (LENGTH, D_MODEL), jnp.float32), -5.0, 5.0)
    return (query_part, key_part)


def draw_queries(key, part):
    return drawn_pair(key)[0].astype(jnp.bfloat16)


def draw_keys(key, part):
    return drawn_pair(key)[1].astype(jnp.bfloat16)


def plant(drawn, own_key, least, largest):
    shape = drawn.shape
    index_at = [jax.random.randint(jax.random.fold_in(own_key, axis), (), 0, shape[axis]) for axis in range(len(shape))]
    drawn = drawn.at[tuple(index_at)].set(least)
    longest = shape.index(max(shape))
    index_at[longest] = (index_at[longest] + 1) % shape[longest]
    return drawn.at[tuple(index_at)].set(largest)


def steps_of(key, dims, shards, least, largest):
    loudness, own = 1.0, jax.random.fold_in(key, 6)
    for dim, shards_of in shards:
        heights = jnp.exp(jax.random.uniform(jax.random.fold_in(own, dim), (shards_of,), jnp.float32, least / len(shards), largest / len(shards)))
        loudness = loudness * jnp.repeat(heights, dims[dim] // shards_of).reshape([-1 if axis == dim else 1 for axis in range(len(dims))])
    return loudness


def length_profile(amount, total, limit, slope):
    portions = [(1 << 20) // math.isqrt(rank ** slope) + 1 for rank in range(2, amount + 1)]
    rest, holding = total - limit - (amount - 1), [1] * (amount - 1)
    while rest > 0:
        candidates = [i for i in range(amount - 1) if holding[i] < limit]
        whole, remaining = sum([portions[i] for i in candidates]), rest
        for i in candidates:
            extra = min(limit - holding[i], max(1, remaining * portions[i] // whole), rest)
            holding[i] = holding[i] + extra
            rest = rest - extra
    return np.array([limit] + holding)


def uneven_parts(own_key, amount, total, limit, lean):
    if amount == 2:
        one = jax.random.randint(own_key, (), max(1, total - limit), min(limit, total - 1) + 1)
        return jnp.stack([one, total - one])
    lengths = jnp.asarray(length_profile(amount, total, limit, lean), jnp.int32)
    pairs = (amount - 1) // 2
    donor, receiver = lengths[1:1 + 2 * pairs:2], lengths[2:2 + 2 * pairs:2]
    margin = jnp.minimum(donor - 1, limit - receiver)
    passed = jax.random.randint(jax.random.fold_in(own_key, 1), (pairs,), 0, 1 << 20) % (margin + 1)
    lengths = lengths.at[1:1 + 2 * pairs:2].set(donor - passed).at[2:2 + 2 * pairs:2].set(receiver + passed)
    return lengths[jax.random.permutation(jax.random.fold_in(own_key, 2), amount)]


def normal_values(rng, extent, deviation, limit, pieces=(), dtype=jnp.bfloat16):
    gain = steps_of(rng, extent, pieces, -0.22, 0.18) if pieces else 1.0
    values = jax.random.normal(rng, extent, jnp.float32) * deviation * gain
    return jnp.minimum(jnp.maximum(values, -limit), limit).astype(dtype)


def setup_inputs(seed: int = 0) -> dict:
    arg_keys = jax.random.split(jax.random.key(seed), 8)
    return {
        "queries": draw_queries(jax.random.fold_in(arg_keys[7], 71), 0),
        "keys": draw_keys(jax.random.fold_in(arg_keys[7], 71), 0),
        "values": normal_values(arg_keys[2], (LENGTH, D_MODEL), 4.0, 16.0, ((0, 16), (1, 8))),
        "out_weight": normal_values(arg_keys[3], (D_MODEL, D_MODEL), D_MODEL ** -0.5, 0.078125, ((0, 8),)),
        "cotangent": normal_values(arg_keys[4], (LENGTH, D_MODEL), 4.0, 16.0, ((0, 16), (1, 8))),
        "contacts": plant((jax.random.randint(arg_keys[5], (NBLOCKS, NBLOCKS), 0, 8) < 1).astype(jnp.int32), jax.random.fold_in(arg_keys[5], 1), 0, 1),
        "chains": jnp.searchsorted(jnp.cumsum(uneven_parts(arg_keys[6], CHAINS, NBLOCKS, NBLOCKS // 2, 2)), jnp.arange(NBLOCKS), side="right").astype(jnp.int32),
    }


NEG = -1e30


def rounded(value):
    return lax.optimization_barrier(value.astype(jnp.bfloat16)).astype(jnp.float32)


def reference(queries, keys, values, out_weight, cotangent, contacts, chains):
    scale = HEAD_SIZE ** -0.5
    allowed = jnp.logical_or(chains[:, None] == chains[None, :], contacts > 0)
    keep = jnp.repeat(jnp.repeat(allowed, BLOCK, axis=0), BLOCK, axis=1)

    def split(field):
        return field.reshape(LENGTH, HEADS, HEAD_SIZE).transpose(1, 0, 2)

    def join(field):
        return field.transpose(1, 0, 2).reshape(LENGTH, D_MODEL)

    q_heads, k_heads, v_heads = split(queries), split(keys), split(values)

    def scores_of(q_one, k_one):
        product = jnp.dot(q_one, k_one.T, preferred_element_type=jnp.float32) * scale
        return jnp.where(keep, product, NEG)

    def forward_head(operands):
        q_one, k_one, v_one = operands
        scores = scores_of(q_one, k_one)
        best = jnp.max(scores, axis=1)
        weights = jnp.where(keep, jnp.exp(scores - best[:, None]), 0.0)
        total = jnp.sum(weights, axis=1)
        mixed_one = jnp.dot(weights.astype(jnp.bfloat16), v_one, preferred_element_type=jnp.float32) / total[:, None]
        return mixed_one.astype(jnp.bfloat16), best + jnp.log(total)

    attended, lse = lax.map(forward_head, (q_heads, k_heads, v_heads))
    mixed = jnp.dot(join(attended), out_weight, preferred_element_type=jnp.float32).astype(jnp.bfloat16)
    grads = lax.dot_general(cotangent, out_weight, (((1,), (1,)), ((), ())), preferred_element_type=jnp.float32).astype(jnp.bfloat16)
    g_heads = split(grads)

    def backward_head(operands):
        q_one, k_one, v_one, g_one, o_one, l_one = operands
        scores = scores_of(q_one, k_one)
        probs = jnp.where(keep, jnp.exp(scores - l_one[:, None]), 0.0)
        delta = jnp.sum(g_one.astype(jnp.float32) * o_one.astype(jnp.float32), axis=1)
        dprob = jnp.dot(g_one, v_one.T, preferred_element_type=jnp.float32)
        dscore = (probs * (dprob - delta[:, None])).astype(jnp.bfloat16)
        dscore_wide = lax.optimization_barrier(dscore).astype(jnp.float32)
        probs_wide = lax.optimization_barrier(probs.astype(jnp.bfloat16)).astype(jnp.float32)
        groups = N_CTX
        q_wide = q_one.astype(jnp.float32).reshape(groups, ROWS_DEV, HEAD_SIZE)
        k_wide = k_one.astype(jnp.float32).reshape(groups, ROWS_DEV, HEAD_SIZE)
        g_wide = g_one.astype(jnp.float32).reshape(groups, ROWS_DEV, HEAD_SIZE)
        q_terms = jnp.einsum("lgr,grd->gld", dscore_wide.reshape(LENGTH, groups, ROWS_DEV), k_wide) * scale
        k_terms = jnp.einsum("grk,grd->gkd", dscore_wide.reshape(groups, ROWS_DEV, LENGTH), q_wide) * scale
        v_terms = jnp.einsum("grk,grd->gkd", probs_wide.reshape(groups, ROWS_DEV, LENGTH), g_wide)
        q_grad = jnp.sum(rounded(q_terms), axis=0).astype(jnp.bfloat16)
        k_grad = jnp.sum(rounded(k_terms), axis=0).astype(jnp.bfloat16)
        v_grad = jnp.sum(rounded(v_terms), axis=0).astype(jnp.bfloat16)
        return q_grad, k_grad, v_grad

    q_grads, k_grads, v_grads = lax.map(backward_head, (q_heads, k_heads, v_heads, g_heads, attended, lse))
    return (mixed, join(q_grads), join(k_grads), join(v_grads))
```

```python
import jax
import jax.numpy as jnp
from jax import lax
from jax.sharding import Mesh
from jax.sharding import PartitionSpec as P

HEAD_SIZE = 128
BLOCK = 128

NEG = -1e30
CTX = ("ctxo", "core")
SWAP = [(0, 1), (1, 0)]


def swap(value):
    return lax.ppermute(value, "core", SWAP)


def pair_rows(own, other, core):
    first = jnp.where(core == 0, own, other)
    second = jnp.where(core == 0, other, own)
    return jnp.concatenate([first, second], axis=0)


def halves(value, core):
    rows = value.shape[0] // 2
    top, bottom = value[:rows], value[rows:]
    own = jnp.where(core == 0, top, bottom)
    other = jnp.where(core == 0, bottom, top)
    return own, other


def per_device(queries, keys, values, out_weight, cotangent, contacts, chains):
    scale = HEAD_SIZE ** (-0.5)
    rows = queries.shape[0]
    size = HEAD_SIZE
    heads = queries.shape[1] // size
    width = heads * size
    n_out = lax.axis_size("ctxo")
    n_head = lax.axis_size("head")
    core = lax.axis_index("core")
    outer = lax.axis_index("ctxo")
    allowed = jnp.logical_or(chains[:, None] == chains[None, :], contacts > 0)
    q_blocks = rows // BLOCK

    spread = jnp.broadcast_to(cotangent[:, None, :], (rows, n_head, width))
    full_cotangent = lax.all_to_all(spread, "head", 1, 1, tiled=True).reshape(rows, n_head * width)
    grads = lax.dot_general(
        full_cotangent, out_weight, (((1,), (1,)), ((), ())), preferred_element_type=jnp.float32
    ).astype(jnp.bfloat16)

    key_half = lax.all_gather(keys, "ctxo", axis=0, tiled=True)
    value_half = lax.all_gather(values, "ctxo", axis=0, tiled=True)
    count = key_half.shape[0]

    q_chip = pair_rows(queries, swap(queries), core)
    chip_rows = 2 * rows
    q_three = q_chip.reshape(chip_rows, heads, size)
    k_three = key_half.reshape(count, heads, size)
    v_three = value_half.reshape(count, heads, size)

    row_blocks = outer * (2 * q_blocks) + jnp.arange(2 * q_blocks)
    shard = 2 * jnp.arange(n_out) + core
    col_blocks = (shard[:, None] * q_blocks + jnp.arange(q_blocks)[None, :]).reshape(-1)
    part_mask = allowed[row_blocks][:, col_blocks]
    keep = jnp.repeat(jnp.repeat(part_mask, BLOCK, axis=0), BLOCK, axis=1)[:, None, :]

    scores = jnp.einsum("qhd,khd->qhk", q_three, k_three, preferred_element_type=jnp.float32) * scale
    scores = jnp.where(keep, scores, NEG)
    best = jnp.max(scores, axis=2)
    weights = jnp.where(keep, jnp.exp(scores - best[:, :, None]), 0.0)
    total = jnp.sum(weights, axis=2)
    accum = jnp.einsum(
        "qhk,khd->qhd", weights.astype(jnp.bfloat16), v_three, preferred_element_type=jnp.float32
    )

    state = jnp.concatenate([best, total, accum.reshape(chip_rows, width)], axis=1)
    own_state, other_state = halves(state, core)
    got_state = swap(other_state)
    best_a, total_a, acc_a = own_state[:, :heads], own_state[:, heads:2 * heads], own_state[:, 2 * heads:]
    best_b, total_b, acc_b = got_state[:, :heads], got_state[:, heads:2 * heads], got_state[:, 2 * heads:]
    best_m = jnp.maximum(best_a, best_b)
    fa = jnp.exp(best_a - best_m)
    fb = jnp.exp(best_b - best_m)
    total_m = total_a * fa + total_b * fb
    acc_m = acc_a.reshape(rows, heads, size) * fa[:, :, None] + acc_b.reshape(rows, heads, size) * fb[:, :, None]
    attended = (acc_m / total_m[:, :, None]).astype(jnp.bfloat16)
    lse = best_m + jnp.log(total_m)

    projected = jnp.dot(attended.reshape(rows, width), out_weight, preferred_element_type=jnp.float32)
    parts = lax.all_to_all(
        projected.astype(jnp.bfloat16).reshape(rows, n_head, width), "head", 1, 1, tiled=True
    )
    mixed = jnp.sum(parts.astype(jnp.float32), axis=1).astype(jnp.bfloat16)

    g_own = grads.reshape(rows, heads, size)
    delta = jnp.sum(g_own.astype(jnp.float32) * attended.astype(jnp.float32), axis=2)
    side = jnp.concatenate([lse, delta], axis=1)
    side_chip = pair_rows(side, swap(side), core)
    lse_chip, delta_chip = side_chip[:, :heads], side_chip[:, heads:]
    g_chip = pair_rows(grads, swap(grads), core).reshape(chip_rows, heads, size)

    scores = jnp.einsum("qhd,khd->qhk", q_three, k_three, preferred_element_type=jnp.float32) * scale
    probs = jnp.where(keep, jnp.exp(scores - lse_chip[:, :, None]), 0.0)
    dprob = jnp.einsum("qhd,khd->qhk", g_chip, v_three, preferred_element_type=jnp.float32)
    dscore = (probs * (dprob - delta_chip[:, :, None])).astype(jnp.bfloat16)

    q_part = jnp.einsum("qhk,khd->qhd", dscore, k_three, preferred_element_type=jnp.float32) * scale
    q_own, q_other = halves(q_part.reshape(chip_rows, width), core)
    query_grad = (q_own + swap(q_other)).astype(jnp.bfloat16)

    key_part = (
        jnp.einsum("qhk,qhd->khd", dscore, q_three, preferred_element_type=jnp.float32) * scale
    ).astype(jnp.bfloat16)
    value_part = jnp.einsum(
        "qhk,qhd->khd", probs.astype(jnp.bfloat16), g_chip, preferred_element_type=jnp.float32
    ).astype(jnp.bfloat16)
    key_grad = lax.psum_scatter(key_part.reshape(count, width), "ctxo", scatter_dimension=0, tiled=True)
    value_grad = lax.psum_scatter(value_part.reshape(count, width), "ctxo", scatter_dimension=0, tiled=True)
    return (mixed, query_grad, key_grad, value_grad)


def solution(mesh):
    devices = mesh.devices
    n_ctx, n_head = devices.shape
    split = Mesh(devices.reshape(n_ctx // 2, 2, n_head), ("ctxo", "core", "head"))
    rows_spec = P(CTX, "head")
    in_specs = (rows_spec, rows_spec, rows_spec, P("head", None), rows_spec, P(), P())
    out_specs = (rows_spec, rows_spec, rows_spec, rows_spec)
    return jax.shard_map(
        per_device, mesh=split, in_specs=in_specs, out_specs=out_specs, check_vma=False
    )
```

```python
import jax
import jax.numpy as jnp
from jax import lax
from jax.sharding import Mesh
from jax.sharding import PartitionSpec as P

HEAD_SIZE = 128
BLOCK = 128

NEG = -1e30
CTX = ("ctxo", "core")
SWAP = [(0, 1), (1, 0)]


def swap(value):
    return lax.ppermute(value, "core", SWAP)


def pair_rows(own, other, core):
    first = jnp.where(core == 0, own, other)
    second = jnp.where(core == 0, other, own)
    return jnp.concatenate([first, second], axis=0)


def halves(value, core):
    rows = value.shape[0] // 2
    top, bottom = value[:rows], value[rows:]
    own = jnp.where(core == 0, top, bottom)
    other = jnp.where(core == 0, bottom, top)
    return own, other


def per_device(queries, keys, values, out_weight, cotangent, contacts, chains):
    scale = HEAD_SIZE ** (-0.5)
    rows = queries.shape[0]
    size = HEAD_SIZE
    heads = queries.shape[1] // size
    width = heads * size
    n_out = lax.axis_size("ctxo")
    n_head = lax.axis_size("head")
    core = lax.axis_index("core")
    outer = lax.axis_index("ctxo")
    allowed = jnp.logical_or(chains[:, None] == chains[None, :], contacts > 0)
    q_blocks = rows // BLOCK

    full_cotangent = lax.all_gather(cotangent, "head", axis=1, tiled=True)
    grads = lax.dot_general(
        full_cotangent, out_weight, (((1,), (1,)), ((), ())), preferred_element_type=jnp.float32
    ).astype(jnp.bfloat16)

    pair = jnp.concatenate([keys, values], axis=1)
    spread = jnp.broadcast_to(pair[None], (n_out,) + pair.shape)
    gathered = lax.all_to_all(spread, "ctxo", 0, 0, tiled=True)
    key_half = gathered[:, :, :width].reshape(n_out * rows, width)
    value_half = gathered[:, :, width:].reshape(n_out * rows, width)
    count = key_half.shape[0]

    q_chip = pair_rows(queries, swap(queries), core)
    chip_rows = 2 * rows
    q_three = q_chip.reshape(chip_rows, heads, size)
    k_three = key_half.reshape(count, heads, size)
    v_three = value_half.reshape(count, heads, size)

    row_blocks = outer * (2 * q_blocks) + jnp.arange(2 * q_blocks)
    shard = 2 * jnp.arange(n_out) + core
    col_blocks = (shard[:, None] * q_blocks + jnp.arange(q_blocks)[None, :]).reshape(-1)
    part_mask = allowed[row_blocks][:, col_blocks]
    keep = jnp.repeat(jnp.repeat(part_mask, BLOCK, axis=0), BLOCK, axis=1)[:, None, :]

    scores = jnp.einsum("qhd,khd->qhk", q_three, k_three, preferred_element_type=jnp.float32) * scale
    scores = jnp.where(keep, scores, NEG)
    best = jnp.max(scores, axis=2)
    weights = jnp.where(keep, jnp.exp(scores - best[:, :, None]), 0.0)
    total = jnp.sum(weights, axis=2)
    accum = jnp.einsum(
        "qhk,khd->qhd", weights.astype(jnp.bfloat16), v_three, preferred_element_type=jnp.float32
    )

    state = jnp.concatenate([best, total, accum.reshape(chip_rows, width)], axis=1)
    own_state, other_state = halves(state, core)
    got_state = swap(other_state)
    best_a, total_a, acc_a = own_state[:, :heads], own_state[:, heads:2 * heads], own_state[:, 2 * heads:]
    best_b, total_b, acc_b = got_state[:, :heads], got_state[:, heads:2 * heads], got_state[:, 2 * heads:]
    best_m = jnp.maximum(best_a, best_b)
    fa = jnp.exp(best_a - best_m)
    fb = jnp.exp(best_b - best_m)
    total_m = total_a * fa + total_b * fb
    acc_m = acc_a.reshape(rows, heads, size) * fa[:, :, None] + acc_b.reshape(rows, heads, size) * fb[:, :, None]
    attended = (acc_m / total_m[:, :, None]).astype(jnp.bfloat16)
    lse = best_m + jnp.log(total_m)

    projected = jnp.dot(attended.reshape(rows, width), out_weight, preferred_element_type=jnp.float32)
    parts = lax.all_to_all(
        projected.astype(jnp.bfloat16).reshape(rows, n_head, width), "head", 1, 1, tiled=True
    )
    mixed = jnp.sum(parts.astype(jnp.float32), axis=1).astype(jnp.bfloat16)

    g_own = grads.reshape(rows, heads, size)
    delta = jnp.sum(g_own.astype(jnp.float32) * attended.astype(jnp.float32), axis=2)
    side = jnp.concatenate([lse, delta], axis=1)
    side_chip = pair_rows(side, swap(side), core)
    lse_chip, delta_chip = side_chip[:, :heads], side_chip[:, heads:]
    g_chip = pair_rows(grads, swap(grads), core).reshape(chip_rows, heads, size)

    scores = jnp.einsum("qhd,khd->qhk", q_three, k_three, preferred_element_type=jnp.float32) * scale
    probs = jnp.where(keep, jnp.exp(scores - lse_chip[:, :, None]), 0.0)
    dprob = jnp.einsum("qhd,khd->qhk", g_chip, v_three, preferred_element_type=jnp.float32)
    dscore = (probs * (dprob - delta_chip[:, :, None])).astype(jnp.bfloat16)

    q_part = jnp.einsum("qhk,khd->qhd", dscore, k_three, preferred_element_type=jnp.float32) * scale
    q_own, q_other = halves(q_part.reshape(chip_rows, width), core)
    query_grad = (q_own + swap(q_other)).astype(jnp.bfloat16)

    key_part = (
        jnp.einsum("qhk,qhd->khd", dscore, q_three, preferred_element_type=jnp.float32) * scale
    ).astype(jnp.bfloat16)
    value_part = jnp.einsum(
        "qhk,qhd->khd", probs.astype(jnp.bfloat16), g_chip, preferred_element_type=jnp.float32
    ).astype(jnp.bfloat16)
    grad_parts = jnp.concatenate(
        [key_part.reshape(count, width), value_part.reshape(count, width)], axis=1
    ).reshape(n_out, rows, 2 * width)
    summed = jnp.sum(lax.all_to_all(grad_parts, "ctxo", 0, 0, tiled=True).astype(jnp.float32), axis=0)
    key_grad = summed[:, :width].astype(jnp.bfloat16)
    value_grad = summed[:, width:].astype(jnp.bfloat16)
    return (mixed, query_grad, key_grad, value_grad)


def solution(mesh):
    devices = mesh.devices
    n_ctx, n_head = devices.shape
    split = Mesh(devices.reshape(n_ctx // 2, 2, n_head), ("ctxo", "core", "head"))
    rows_spec = P(CTX, "head")
    in_specs = (rows_spec, rows_spec, rows_spec, P("head", None), rows_spec, P(), P())
    out_specs = (rows_spec, rows_spec, rows_spec, rows_spec)
    return jax.shard_map(
        per_device, mesh=split, in_specs=in_specs, out_specs=out_specs, check_vma=False
    )
```

```python
import jax
import jax.numpy as jnp
from jax import lax
from jax.sharding import Mesh
from jax.sharding import PartitionSpec as P

HEAD_SIZE = 128
BLOCK = 128

NEG = -1e30
CTX = ("ctxo", "core")
SWAP = [(0, 1), (1, 0)]
GROUPS = ((0, 1), (1, 3), (3, 5))


def swap(value):
    return lax.ppermute(value, "core", SWAP)


def pair_rows(own, other, core):
    first = jnp.where(core == 0, own, other)
    second = jnp.where(core == 0, other, own)
    return jnp.concatenate([first, second], axis=0)


def halves(value, core):
    rows = value.shape[0] // 2
    top, bottom = value[:rows], value[rows:]
    own = jnp.where(core == 0, top, bottom)
    other = jnp.where(core == 0, bottom, top)
    return own, other


def per_device(queries, keys, values, out_weight, cotangent, contacts, chains):
    scale = HEAD_SIZE ** (-0.5)
    rows = queries.shape[0]
    size = HEAD_SIZE
    heads = queries.shape[1] // size
    width = heads * size
    n_out = lax.axis_size("ctxo")
    core = lax.axis_index("core")
    outer = lax.axis_index("ctxo")
    allowed = jnp.logical_or(chains[:, None] == chains[None, :], contacts > 0)
    q_blocks = rows // BLOCK
    chip_rows = 2 * rows
    count = n_out * rows

    full_cotangent = lax.all_gather(cotangent, "head", axis=1, tiled=True)
    grads = lax.dot_general(
        full_cotangent, out_weight, (((1,), (1,)), ((), ())), preferred_element_type=jnp.float32
    ).astype(jnp.bfloat16)

    q_chip = pair_rows(queries, swap(queries), core).reshape(chip_rows, heads, size)
    g_chip = pair_rows(grads, swap(grads), core).reshape(chip_rows, heads, size)
    g_own = grads.reshape(rows, heads, size)

    row_blocks = outer * (2 * q_blocks) + jnp.arange(2 * q_blocks)
    shard = 2 * jnp.arange(n_out) + core
    col_blocks = (shard[:, None] * q_blocks + jnp.arange(q_blocks)[None, :]).reshape(-1)
    part_mask = allowed[row_blocks][:, col_blocks]
    keep = jnp.repeat(jnp.repeat(part_mask, BLOCK, axis=0), BLOCK, axis=1)[:, None, :]

    attended_parts, lse_parts, kv_parts = [], [], []
    for lo, hi in GROUPS:
        span = hi - lo
        cols = slice(lo * size, hi * size)
        pair = jnp.stack([keys[:, cols], values[:, cols]])
        spread = jnp.broadcast_to(pair[None], (n_out,) + pair.shape)
        gathered = lax.all_to_all(spread, "ctxo", 0, 0, tiled=True)
        k_three = gathered[:, 0].reshape(count, span, size)
        v_three = gathered[:, 1].reshape(count, span, size)
        kv_parts.append((k_three, v_three))
        q_three = q_chip[:, lo:hi]

        scores = jnp.einsum("qhd,khd->qhk", q_three, k_three, preferred_element_type=jnp.float32) * scale
        scores = jnp.where(keep, scores, NEG)
        best = jnp.max(scores, axis=2)
        weights = jnp.where(keep, jnp.exp(scores - best[:, :, None]), 0.0)
        total = jnp.sum(weights, axis=2)
        accum = jnp.einsum(
            "qhk,khd->qhd", weights.astype(jnp.bfloat16), v_three, preferred_element_type=jnp.float32
        )

        state = jnp.concatenate([best, total, accum.reshape(chip_rows, span * size)], axis=1)
        own_state, other_state = halves(state, core)
        got_state = swap(other_state)
        best_a, total_a, acc_a = own_state[:, :span], own_state[:, span:2 * span], own_state[:, 2 * span:]
        best_b, total_b, acc_b = got_state[:, :span], got_state[:, span:2 * span], got_state[:, 2 * span:]
        best_m = jnp.maximum(best_a, best_b)
        fa = jnp.exp(best_a - best_m)
        fb = jnp.exp(best_b - best_m)
        total_m = total_a * fa + total_b * fb
        acc_m = (
            acc_a.reshape(rows, span, size) * fa[:, :, None]
            + acc_b.reshape(rows, span, size) * fb[:, :, None]
        )
        attended_parts.append((acc_m / total_m[:, :, None]).astype(jnp.bfloat16))
        lse_parts.append(best_m + jnp.log(total_m))

    attended = jnp.concatenate(attended_parts, axis=1)

    n_head = lax.axis_size("head")
    projected = jnp.dot(attended.reshape(rows, width), out_weight, preferred_element_type=jnp.float32)
    parts = lax.all_to_all(
        projected.astype(jnp.bfloat16).reshape(rows, n_head, width), "head", 1, 1, tiled=True
    )
    mixed = jnp.sum(parts.astype(jnp.float32), axis=1).astype(jnp.bfloat16)

    q_grads, k_grads, v_grads = [], [], []
    for (lo, hi), att, lse, (k_three, v_three) in zip(GROUPS, attended_parts, lse_parts, kv_parts):
        span = hi - lo
        q_three = q_chip[:, lo:hi]
        g_three = g_chip[:, lo:hi]
        delta = jnp.sum(g_own[:, lo:hi].astype(jnp.float32) * att.astype(jnp.float32), axis=2)
        side = jnp.concatenate([lse, delta], axis=1)
        side_chip = pair_rows(side, swap(side), core)
        lse_chip, delta_chip = side_chip[:, :span], side_chip[:, span:]

        scores = jnp.einsum("qhd,khd->qhk", q_three, k_three, preferred_element_type=jnp.float32) * scale
        probs = jnp.where(keep, jnp.exp(scores - lse_chip[:, :, None]), 0.0)
        dprob = jnp.einsum("qhd,khd->qhk", g_three, v_three, preferred_element_type=jnp.float32)
        dscore = (probs * (dprob - delta_chip[:, :, None])).astype(jnp.bfloat16)

        q_part = jnp.einsum("qhk,khd->qhd", dscore, k_three, preferred_element_type=jnp.float32) * scale
        q_own, q_other = halves(q_part.reshape(chip_rows, span * size), core)
        q_grads.append((q_own + swap(q_other)).astype(jnp.bfloat16))

        key_part = (
            jnp.einsum("qhk,qhd->khd", dscore, q_three, preferred_element_type=jnp.float32) * scale
        ).astype(jnp.bfloat16)
        value_part = jnp.einsum(
            "qhk,qhd->khd", probs.astype(jnp.bfloat16), g_three, preferred_element_type=jnp.float32
        ).astype(jnp.bfloat16)
        grad_parts = jnp.stack(
            [key_part.reshape(n_out, rows, span * size), value_part.reshape(n_out, rows, span * size)],
            axis=1,
        )
        summed = jnp.sum(
            lax.all_to_all(grad_parts, "ctxo", 0, 0, tiled=True).astype(jnp.float32), axis=0
        )
        k_grads.append(summed[0].astype(jnp.bfloat16))
        v_grads.append(summed[1].astype(jnp.bfloat16))

    query_grad = jnp.concatenate(q_grads, axis=1)
    key_grad = jnp.concatenate(k_grads, axis=1)
    value_grad = jnp.concatenate(v_grads, axis=1)
    return (mixed, query_grad, key_grad, value_grad)


def solution(mesh):
    devices = mesh.devices
    n_ctx, n_head = devices.shape
    split = Mesh(devices.reshape(n_ctx // 2, 2, n_head), ("ctxo", "core", "head"))
    rows_spec = P(CTX, "head")
    in_specs = (rows_spec, rows_spec, rows_spec, P("head", None), rows_spec, P(), P())
    out_specs = (rows_spec, rows_spec, rows_spec, rows_spec)
    return jax.shard_map(
        per_device, mesh=split, in_specs=in_specs, out_specs=out_specs, check_vma=False
    )
```

```python
import jax
import jax.numpy as jnp
from jax import lax
from jax.sharding import Mesh
from jax.sharding import PartitionSpec as P

HEAD_SIZE = 128
BLOCK = 128

NEG = -1e30
CTX = ("ctxo", "core")
SWAP = [(0, 1), (1, 0)]


def swap(value):
    return lax.ppermute(value, "core", SWAP)


def shift(value, step, count):
    return lax.ppermute(value, "ctxo", [(i, (i + step) % count) for i in range(count)])


def pair_rows(own, other, core):
    first = jnp.where(core == 0, own, other)
    second = jnp.where(core == 0, other, own)
    return jnp.concatenate([first, second], axis=0)


def halves(value, core):
    rows = value.shape[0] // 2
    top, bottom = value[:rows], value[rows:]
    own = jnp.where(core == 0, top, bottom)
    other = jnp.where(core == 0, bottom, top)
    return own, other


def per_device(queries, keys, values, out_weight, cotangent, contacts, chains):
    scale = HEAD_SIZE ** (-0.5)
    rows = queries.shape[0]
    size = HEAD_SIZE
    heads = queries.shape[1] // size
    width = heads * size
    n_out = lax.axis_size("ctxo")
    n_head = lax.axis_size("head")
    core = lax.axis_index("core")
    outer = lax.axis_index("ctxo")
    allowed = jnp.logical_or(chains[:, None] == chains[None, :], contacts > 0)
    q_blocks = rows // BLOCK
    chip_rows = 2 * rows

    pair = jnp.stack([keys, values])
    shards = [pair] + [shift(pair, s, n_out) for s in range(1, n_out)]

    full_cotangent = lax.all_gather(cotangent, "head", axis=1, tiled=True)
    grads = lax.dot_general(
        full_cotangent, out_weight, (((1,), (1,)), ((), ())), preferred_element_type=jnp.float32
    ).astype(jnp.bfloat16)

    q_three = pair_rows(queries, swap(queries), core).reshape(chip_rows, heads, size)

    row_blocks = outer * (2 * q_blocks) + jnp.arange(2 * q_blocks)
    row_mask = allowed[row_blocks]

    def keep_of(s):
        source = (outer - s) % n_out
        cols = (2 * source + core) * q_blocks + jnp.arange(q_blocks)
        part = row_mask[:, cols]
        return jnp.repeat(jnp.repeat(part, BLOCK, axis=0), BLOCK, axis=1)[:, None, :]

    keeps = [keep_of(s) for s in range(n_out)]

    best = jnp.full((chip_rows, heads), NEG, jnp.float32)
    total = jnp.zeros((chip_rows, heads), jnp.float32)
    accum = jnp.zeros((chip_rows, heads, size), jnp.float32)
    for s in range(n_out):
        k_three = shards[s][0].reshape(rows, heads, size)
        v_three = shards[s][1].reshape(rows, heads, size)
        keep = keeps[s]
        scores = jnp.einsum("qhd,khd->qhk", q_three, k_three, preferred_element_type=jnp.float32) * scale
        scores = jnp.where(keep, scores, NEG)
        best_new = jnp.maximum(best, jnp.max(scores, axis=2))
        weights = jnp.where(keep, jnp.exp(scores - best_new[:, :, None]), 0.0)
        fix = jnp.exp(best - best_new)
        total = total * fix + jnp.sum(weights, axis=2)
        accum = accum * fix[:, :, None] + jnp.einsum(
            "qhk,khd->qhd", weights.astype(jnp.bfloat16), v_three, preferred_element_type=jnp.float32
        )
        best = best_new

    state = jnp.concatenate([best, total, accum.reshape(chip_rows, width)], axis=1)
    own_state, other_state = halves(state, core)
    got_state = swap(other_state)
    best_a, total_a, acc_a = own_state[:, :heads], own_state[:, heads:2 * heads], own_state[:, 2 * heads:]
    best_b, total_b, acc_b = got_state[:, :heads], got_state[:, heads:2 * heads], got_state[:, 2 * heads:]
    best_m = jnp.maximum(best_a, best_b)
    fa = jnp.exp(best_a - best_m)
    fb = jnp.exp(best_b - best_m)
    total_m = total_a * fa + total_b * fb
    acc_m = acc_a.reshape(rows, heads, size) * fa[:, :, None] + acc_b.reshape(rows, heads, size) * fb[:, :, None]
    attended = (acc_m / total_m[:, :, None]).astype(jnp.bfloat16)
    lse = best_m + jnp.log(total_m)

    projected = jnp.dot(attended.reshape(rows, width), out_weight, preferred_element_type=jnp.float32)
    parts = lax.all_to_all(
        projected.astype(jnp.bfloat16).reshape(rows, n_head, width), "head", 1, 1, tiled=True
    )
    mixed = jnp.sum(parts.astype(jnp.float32), axis=1).astype(jnp.bfloat16)

    g_own = grads.reshape(rows, heads, size)
    delta = jnp.sum(g_own.astype(jnp.float32) * attended.astype(jnp.float32), axis=2)
    side = jnp.concatenate([lse, delta], axis=1)
    side_chip = pair_rows(side, swap(side), core)
    lse_chip, delta_chip = side_chip[:, :heads], side_chip[:, heads:]
    g_three = pair_rows(grads, swap(grads), core).reshape(chip_rows, heads, size)

    q_accum = jnp.zeros((chip_rows, heads, size), jnp.float32)
    kv_sum = None
    for s in range(n_out):
        k_three = shards[s][0].reshape(rows, heads, size)
        v_three = shards[s][1].reshape(rows, heads, size)
        keep = keeps[s]
        scores = jnp.einsum("qhd,khd->qhk", q_three, k_three, preferred_element_type=jnp.float32) * scale
        probs = jnp.where(keep, jnp.exp(scores - lse_chip[:, :, None]), 0.0)
        dprob = jnp.einsum("qhd,khd->qhk", g_three, v_three, preferred_element_type=jnp.float32)
        dscore = (probs * (dprob - delta_chip[:, :, None])).astype(jnp.bfloat16)
        q_term = jnp.einsum("qhk,khd->qhd", dscore, k_three, preferred_element_type=jnp.float32) * scale
        q_accum = q_accum + q_term.astype(jnp.bfloat16).astype(jnp.float32)
        key_part = (
            jnp.einsum("qhk,qhd->khd", dscore, q_three, preferred_element_type=jnp.float32) * scale
        ).astype(jnp.bfloat16)
        value_part = jnp.einsum(
            "qhk,qhd->khd", probs.astype(jnp.bfloat16), g_three, preferred_element_type=jnp.float32
        ).astype(jnp.bfloat16)
        term = jnp.stack([key_part.reshape(rows, width), value_part.reshape(rows, width)])
        if s:
            term = shift(term, n_out - s, n_out)
        term = term.astype(jnp.float32)
        kv_sum = term if kv_sum is None else kv_sum + term

    q_own, q_other = halves(q_accum.reshape(chip_rows, width), core)
    query_grad = (q_own + swap(q_other)).astype(jnp.bfloat16)
    key_grad = kv_sum[0].astype(jnp.bfloat16)
    value_grad = kv_sum[1].astype(jnp.bfloat16)
    return (mixed, query_grad, key_grad, value_grad)


def solution(mesh):
    devices = mesh.devices
    n_ctx, n_head = devices.shape
    split = Mesh(devices.reshape(n_ctx // 2, 2, n_head), ("ctxo", "core", "head"))
    rows_spec = P(CTX, "head")
    in_specs = (rows_spec, rows_spec, rows_spec, P("head", None), rows_spec, P(), P())
    out_specs = (rows_spec, rows_spec, rows_spec, rows_spec)
    return jax.shard_map(
        per_device, mesh=split, in_specs=in_specs, out_specs=out_specs, check_vma=False
    )
```

```python
import jax
import jax.numpy as jnp
from jax import lax
from jax.sharding import Mesh
from jax.sharding import PartitionSpec as P

HEAD_SIZE = 128
BLOCK = 128

NEG = -1e30
CTX = ("ctxo", "core")
SWAP = [(0, 1), (1, 0)]
GROUPS = ((0, 1), (1, 3), (3, 5))


def swap(value):
    return lax.ppermute(value, "core", SWAP)


def pair_rows(own, other, core):
    first = jnp.where(core == 0, own, other)
    second = jnp.where(core == 0, other, own)
    return jnp.concatenate([first, second], axis=0)


def halves(value, core):
    rows = value.shape[0] // 2
    top, bottom = value[:rows], value[rows:]
    own = jnp.where(core == 0, top, bottom)
    other = jnp.where(core == 0, bottom, top)
    return own, other


def per_device(queries, keys, values, out_weight, cotangent, contacts, chains):
    scale = HEAD_SIZE ** (-0.5)
    rows = queries.shape[0]
    size = HEAD_SIZE
    heads = queries.shape[1] // size
    width = heads * size
    n_out = lax.axis_size("ctxo")
    core = lax.axis_index("core")
    outer = lax.axis_index("ctxo")
    allowed = jnp.logical_or(chains[:, None] == chains[None, :], contacts > 0)
    q_blocks = rows // BLOCK
    chip_rows = 2 * rows
    count = n_out * rows

    full_cotangent = lax.all_gather(cotangent, "head", axis=1, tiled=True)
    grads = lax.dot_general(
        full_cotangent, out_weight, (((1,), (1,)), ((), ())), preferred_element_type=jnp.float32
    ).astype(jnp.bfloat16)

    q_chip = pair_rows(queries, swap(queries), core).reshape(chip_rows, heads, size)
    g_chip = pair_rows(grads, swap(grads), core).reshape(chip_rows, heads, size)
    g_own = grads.reshape(rows, heads, size)

    row_blocks = outer * (2 * q_blocks) + jnp.arange(2 * q_blocks)
    shard = 2 * jnp.arange(n_out) + core
    col_blocks = (shard[:, None] * q_blocks + jnp.arange(q_blocks)[None, :]).reshape(-1)
    part_mask = allowed[row_blocks][:, col_blocks]
    keep = jnp.repeat(jnp.repeat(part_mask, BLOCK, axis=0), BLOCK, axis=1)[:, None, :]

    attended_parts, lse_parts, kv_parts = [], [], []
    for lo, hi in GROUPS:
        span = hi - lo
        cols = slice(lo * size, hi * size)
        pair = jnp.stack([keys[:, cols], values[:, cols]])
        spread = jnp.broadcast_to(pair[None], (n_out,) + pair.shape)
        gathered = lax.all_to_all(spread, "ctxo", 0, 0, tiled=True)
        k_three = gathered[:, 0].reshape(count, span, size)
        v_three = gathered[:, 1].reshape(count, span, size)
        kv_parts.append((k_three, v_three))
        q_three = q_chip[:, lo:hi]

        scores = jnp.einsum("qhd,khd->qhk", q_three, k_three, preferred_element_type=jnp.float32) * scale
        scores = jnp.where(keep, scores, NEG)
        best = jnp.max(scores, axis=2)
        weights = jnp.where(keep, jnp.exp(scores - best[:, :, None]), 0.0)
        total = jnp.sum(weights, axis=2)
        accum = jnp.einsum(
            "qhk,khd->qhd", weights.astype(jnp.bfloat16), v_three, preferred_element_type=jnp.float32
        )

        state = jnp.concatenate([best, total, accum.reshape(chip_rows, span * size)], axis=1)
        own_state, other_state = halves(state, core)
        got_state = swap(other_state)
        best_a, total_a, acc_a = own_state[:, :span], own_state[:, span:2 * span], own_state[:, 2 * span:]
        best_b, total_b, acc_b = got_state[:, :span], got_state[:, span:2 * span], got_state[:, 2 * span:]
        best_m = jnp.maximum(best_a, best_b)
        fa = jnp.exp(best_a - best_m)
        fb = jnp.exp(best_b - best_m)
        total_m = total_a * fa + total_b * fb
        acc_m = (
            acc_a.reshape(rows, span, size) * fa[:, :, None]
            + acc_b.reshape(rows, span, size) * fb[:, :, None]
        )
        attended_parts.append((acc_m / total_m[:, :, None]).astype(jnp.bfloat16))
        lse_parts.append(best_m + jnp.log(total_m))

    attended = jnp.concatenate(attended_parts, axis=1)

    projected = jnp.dot(attended.reshape(rows, width), out_weight, preferred_element_type=jnp.float32)
    mixed = lax.psum_scatter(projected.astype(jnp.bfloat16), "head", scatter_dimension=1, tiled=True)

    q_grads, k_grads, v_grads = [], [], []
    for (lo, hi), att, lse, (k_three, v_three) in zip(GROUPS, attended_parts, lse_parts, kv_parts):
        span = hi - lo
        q_three = q_chip[:, lo:hi]
        g_three = g_chip[:, lo:hi]
        delta = jnp.sum(g_own[:, lo:hi].astype(jnp.float32) * att.astype(jnp.float32), axis=2)
        side = jnp.concatenate([lse, delta], axis=1)
        side_chip = pair_rows(side, swap(side), core)
        lse_chip, delta_chip = side_chip[:, :span], side_chip[:, span:]

        scores = jnp.einsum("qhd,khd->qhk", q_three, k_three, preferred_element_type=jnp.float32) * scale
        probs = jnp.where(keep, jnp.exp(scores - lse_chip[:, :, None]), 0.0)
        dprob = jnp.einsum("qhd,khd->qhk", g_three, v_three, preferred_element_type=jnp.float32)
        dscore = (probs * (dprob - delta_chip[:, :, None])).astype(jnp.bfloat16)

        q_part = jnp.einsum("qhk,khd->qhd", dscore, k_three, preferred_element_type=jnp.float32) * scale
        q_own, q_other = halves(q_part.reshape(chip_rows, span * size), core)
        q_grads.append((q_own + swap(q_other)).astype(jnp.bfloat16))

        key_part = (
            jnp.einsum("qhk,qhd->khd", dscore, q_three, preferred_element_type=jnp.float32) * scale
        ).astype(jnp.bfloat16)
        value_part = jnp.einsum(
            "qhk,qhd->khd", probs.astype(jnp.bfloat16), g_three, preferred_element_type=jnp.float32
        ).astype(jnp.bfloat16)
        grad_parts = jnp.stack(
            [key_part.reshape(n_out, rows, span * size), value_part.reshape(n_out, rows, span * size)],
            axis=1,
        )
        summed = jnp.sum(
            lax.all_to_all(grad_parts, "ctxo", 0, 0, tiled=True).astype(jnp.float32), axis=0
        )
        k_grads.append(summed[0].astype(jnp.bfloat16))
        v_grads.append(summed[1].astype(jnp.bfloat16))

    query_grad = jnp.concatenate(q_grads, axis=1)
    key_grad = jnp.concatenate(k_grads, axis=1)
    value_grad = jnp.concatenate(v_grads, axis=1)
    return (mixed, query_grad, key_grad, value_grad)


def solution(mesh):
    devices = mesh.devices
    n_ctx, n_head = devices.shape
    split = Mesh(devices.reshape(n_ctx // 2, 2, n_head), ("ctxo", "core", "head"))
    rows_spec = P(CTX, "head")
    in_specs = (rows_spec, rows_spec, rows_spec, P("head", None), rows_spec, P(), P())
    out_specs = (rows_spec, rows_spec, rows_spec, rows_spec)
    return jax.shard_map(
        per_device, mesh=split, in_specs=in_specs, out_specs=out_specs, check_vma=False
    )
```

```python
import jax
import jax.numpy as jnp
from jax import lax
from jax.sharding import Mesh
from jax.sharding import PartitionSpec as P

HEAD_SIZE = 128
BLOCK = 128

NEG = -1e30
CTX = ("ctxo", "core")
SWAP = [(0, 1), (1, 0)]
GROUPS = ((0, 1), (1, 3), (3, 5))


def swap(value):
    return lax.ppermute(value, "core", SWAP)


def pair_rows(own, other, core):
    first = jnp.where(core == 0, own, other)
    second = jnp.where(core == 0, other, own)
    return jnp.concatenate([first, second], axis=0)


def halves(value, core):
    rows = value.shape[0] // 2
    top, bottom = value[:rows], value[rows:]
    own = jnp.where(core == 0, top, bottom)
    other = jnp.where(core == 0, bottom, top)
    return own, other


def per_device(queries, keys, values, out_weight, cotangent, contacts, chains):
    scale = HEAD_SIZE ** (-0.5)
    rows = queries.shape[0]
    size = HEAD_SIZE
    heads = queries.shape[1] // size
    width = heads * size
    n_out = lax.axis_size("ctxo")
    core = lax.axis_index("core")
    outer = lax.axis_index("ctxo")
    allowed = jnp.logical_or(chains[:, None] == chains[None, :], contacts > 0)
    q_blocks = rows // BLOCK
    chip_rows = 2 * rows
    count = n_out * rows

    full_cotangent = lax.all_gather(cotangent, "head", axis=1, tiled=True)
    grads = lax.dot_general(
        full_cotangent, out_weight, (((1,), (1,)), ((), ())), preferred_element_type=jnp.float32
    ).astype(jnp.bfloat16)

    q_chip = pair_rows(queries, swap(queries), core).reshape(chip_rows, heads, size)
    g_chip = pair_rows(grads, swap(grads), core).reshape(chip_rows, heads, size)
    g_own = grads.reshape(rows, heads, size)

    row_blocks = outer * (2 * q_blocks) + jnp.arange(2 * q_blocks)
    shard = 2 * jnp.arange(n_out) + core
    col_blocks = (shard[:, None] * q_blocks + jnp.arange(q_blocks)[None, :]).reshape(-1)
    part_mask = allowed[row_blocks][:, col_blocks]
    keep = jnp.repeat(jnp.repeat(part_mask, BLOCK, axis=0), BLOCK, axis=1)[:, None, :]

    attended_parts, lse_parts, kv_parts = [], [], []
    for lo, hi in GROUPS:
        span = hi - lo
        cols = slice(lo * size, hi * size)
        pair = jnp.stack([keys[:, cols], values[:, cols]])
        if lo == 0:
            gathered = lax.all_gather(pair, "ctxo", axis=0)
        else:
            spread = jnp.broadcast_to(pair[None], (n_out,) + pair.shape)
            gathered = lax.all_to_all(spread, "ctxo", 0, 0, tiled=True)
        k_three = gathered[:, 0].reshape(count, span, size)
        v_three = gathered[:, 1].reshape(count, span, size)
        kv_parts.append((k_three, v_three))
        q_three = q_chip[:, lo:hi]

        scores = jnp.einsum("qhd,khd->qhk", q_three, k_three, preferred_element_type=jnp.float32) * scale
        scores = jnp.where(keep, scores, NEG)
        best = jnp.max(scores, axis=2)
        weights = jnp.where(keep, jnp.exp(scores - best[:, :, None]), 0.0)
        total = jnp.sum(weights, axis=2)
        accum = jnp.einsum(
            "qhk,khd->qhd", weights.astype(jnp.bfloat16), v_three, preferred_element_type=jnp.float32
        )

        state = jnp.concatenate([best, total, accum.reshape(chip_rows, span * size)], axis=1)
        own_state, other_state = halves(state, core)
        got_state = swap(other_state)
        best_a, total_a, acc_a = own_state[:, :span], own_state[:, span:2 * span], own_state[:, 2 * span:]
        best_b, total_b, acc_b = got_state[:, :span], got_state[:, span:2 * span], got_state[:, 2 * span:]
        best_m = jnp.maximum(best_a, best_b)
        fa = jnp.exp(best_a - best_m)
        fb = jnp.exp(best_b - best_m)
        total_m = total_a * fa + total_b * fb
        acc_m = (
            acc_a.reshape(rows, span, size) * fa[:, :, None]
            + acc_b.reshape(rows, span, size) * fb[:, :, None]
        )
        attended_parts.append((acc_m / total_m[:, :, None]).astype(jnp.bfloat16))
        lse_parts.append(best_m + jnp.log(total_m))

    attended = jnp.concatenate(attended_parts, axis=1)

    projected = jnp.dot(attended.reshape(rows, width), out_weight, preferred_element_type=jnp.float32)
    mixed = lax.psum_scatter(projected.astype(jnp.bfloat16), "head", scatter_dimension=1, tiled=True)

    q_grads, k_grads, v_grads = [], [], []
    for (lo, hi), att, lse, (k_three, v_three) in zip(GROUPS, attended_parts, lse_parts, kv_parts):
        span = hi - lo
        q_three = q_chip[:, lo:hi]
        g_three = g_chip[:, lo:hi]
        delta = jnp.sum(g_own[:, lo:hi].astype(jnp.float32) * att.astype(jnp.float32), axis=2)
        side = jnp.concatenate([lse, delta], axis=1)
        side_chip = pair_rows(side, swap(side), core)
        lse_chip, delta_chip = side_chip[:, :span], side_chip[:, span:]

        scores = jnp.einsum("qhd,khd->qhk", q_three, k_three, preferred_element_type=jnp.float32) * scale
        probs = jnp.where(keep, jnp.exp(scores - lse_chip[:, :, None]), 0.0)
        dprob = jnp.einsum("qhd,khd->qhk", g_three, v_three, preferred_element_type=jnp.float32)
        dscore = (probs * (dprob - delta_chip[:, :, None])).astype(jnp.bfloat16)

        q_part = jnp.einsum("qhk,khd->qhd", dscore, k_three, preferred_element_type=jnp.float32) * scale
        q_own, q_other = halves(q_part.reshape(chip_rows, span * size), core)
        q_grads.append((q_own + swap(q_other)).astype(jnp.bfloat16))

        key_part = (
            jnp.einsum("qhk,qhd->khd", dscore, q_three, preferred_element_type=jnp.float32) * scale
        ).astype(jnp.bfloat16)
        value_part = jnp.einsum(
            "qhk,qhd->khd", probs.astype(jnp.bfloat16), g_three, preferred_element_type=jnp.float32
        ).astype(jnp.bfloat16)
        grad_parts = jnp.stack(
            [key_part.reshape(n_out, rows, span * size), value_part.reshape(n_out, rows, span * size)],
            axis=1,
        )
        summed = jnp.sum(
            lax.all_to_all(grad_parts, "ctxo", 0, 0, tiled=True).astype(jnp.float32), axis=0
        )
        k_grads.append(summed[0].astype(jnp.bfloat16))
        v_grads.append(summed[1].astype(jnp.bfloat16))

    query_grad = jnp.concatenate(q_grads, axis=1)
    key_grad = jnp.concatenate(k_grads, axis=1)
    value_grad = jnp.concatenate(v_grads, axis=1)
    return (mixed, query_grad, key_grad, value_grad)


def solution(mesh):
    devices = mesh.devices
    n_ctx, n_head = devices.shape
    split = Mesh(devices.reshape(n_ctx // 2, 2, n_head), ("ctxo", "core", "head"))
    rows_spec = P(CTX, "head")
    in_specs = (rows_spec, rows_spec, rows_spec, P("head", None), rows_spec, P(), P())
    out_specs = (rows_spec, rows_spec, rows_spec, rows_spec)
    return jax.shard_map(
        per_device, mesh=split, in_specs=in_specs, out_specs=out_specs, check_vma=False
    )
```

```python
import jax
import jax.numpy as jnp
from jax import lax
from jax.sharding import Mesh
from jax.sharding import PartitionSpec as P

HEAD_SIZE = 128
BLOCK = 128

NEG = -1e30
CTX = ("ctxo", "core")
SWAP = [(0, 1), (1, 0)]


def swap(value):
    return lax.ppermute(value, "core", SWAP)


def pair_rows(own, other, core):
    first = jnp.where(core == 0, own, other)
    second = jnp.where(core == 0, other, own)
    return jnp.concatenate([first, second], axis=0)


def halves(value, core):
    rows = value.shape[0] // 2
    top, bottom = value[:rows], value[rows:]
    own = jnp.where(core == 0, top, bottom)
    other = jnp.where(core == 0, bottom, top)
    return own, other


def merged(value, core):
    own, other = halves(value, core)
    return own + swap(other)


def gather_chips(value, n_out):
    spread = jnp.broadcast_to(value[None], (n_out,) + value.shape)
    return lax.all_to_all(spread, "ctxo", 0, 0, tiled=True)


def per_device(queries, keys, values, out_weight, cotangent, contacts, chains):
    scale = HEAD_SIZE ** (-0.5)
    rows = queries.shape[0]
    size = HEAD_SIZE
    heads = queries.shape[1] // size
    width = heads * size
    n_out = lax.axis_size("ctxo")
    core = lax.axis_index("core")
    outer = lax.axis_index("ctxo")
    allowed = jnp.logical_or(chains[:, None] == chains[None, :], contacts > 0)
    q_blocks = rows // BLOCK
    chip_rows = 2 * rows
    count = n_out * rows

    gathered = gather_chips(jnp.stack([keys, values]), n_out)
    k_half = gathered[:, 0].reshape(count, heads, size)
    v_half = gathered[:, 1].reshape(count, heads, size)
    q_half = lax.all_gather(queries, "ctxo", axis=0).reshape(count, heads, size)

    full_cotangent = lax.all_gather(cotangent, "head", axis=1, tiled=True)
    grads = lax.dot_general(
        full_cotangent, out_weight, (((1,), (1,)), ((), ())), preferred_element_type=jnp.float32
    ).astype(jnp.bfloat16)
    g_half = gather_chips(grads, n_out).reshape(count, heads, size)

    q_chip = pair_rows(queries, swap(queries), core).reshape(chip_rows, heads, size)
    g_chip = pair_rows(grads, swap(grads), core).reshape(chip_rows, heads, size)
    k_chip = pair_rows(keys, swap(keys), core).reshape(chip_rows, heads, size)
    v_chip = pair_rows(values, swap(values), core).reshape(chip_rows, heads, size)

    chip_blocks = outer * (2 * q_blocks) + jnp.arange(2 * q_blocks)
    shard = 2 * jnp.arange(n_out) + core
    half_blocks = (shard[:, None] * q_blocks + jnp.arange(q_blocks)[None, :]).reshape(-1)

    def expand(part):
        return jnp.repeat(jnp.repeat(part, BLOCK, axis=0), BLOCK, axis=1)[:, None, :]

    keep = expand(allowed[chip_blocks][:, half_blocks])
    keep_keys = expand(allowed[half_blocks][:, chip_blocks])

    scores = jnp.einsum("qhd,khd->qhk", q_chip, k_half, preferred_element_type=jnp.float32) * scale
    scores = jnp.where(keep, scores, NEG)
    best = jnp.max(scores, axis=2)
    weights = jnp.where(keep, jnp.exp(scores - best[:, :, None]), 0.0)
    total = jnp.sum(weights, axis=2)
    accum = jnp.einsum(
        "qhk,khd->qhd", weights.astype(jnp.bfloat16), v_half, preferred_element_type=jnp.float32
    )

    state = jnp.concatenate([best, total, accum.reshape(chip_rows, width)], axis=1)
    own_state, other_state = halves(state, core)
    got_state = swap(other_state)
    best_a, total_a, acc_a = own_state[:, :heads], own_state[:, heads:2 * heads], own_state[:, 2 * heads:]
    best_b, total_b, acc_b = got_state[:, :heads], got_state[:, heads:2 * heads], got_state[:, 2 * heads:]
    best_m = jnp.maximum(best_a, best_b)
    fa = jnp.exp(best_a - best_m)
    fb = jnp.exp(best_b - best_m)
    total_m = total_a * fa + total_b * fb
    acc_m = acc_a.reshape(rows, heads, size) * fa[:, :, None] + acc_b.reshape(rows, heads, size) * fb[:, :, None]
    attended = (acc_m / total_m[:, :, None]).astype(jnp.bfloat16)
    lse = best_m + jnp.log(total_m)

    projected = jnp.dot(attended.reshape(rows, width), out_weight, preferred_element_type=jnp.float32)
    mixed = lax.psum_scatter(projected.astype(jnp.bfloat16), "head", scatter_dimension=1, tiled=True)

    g_own = grads.reshape(rows, heads, size)
    delta = jnp.sum(g_own.astype(jnp.float32) * attended.astype(jnp.float32), axis=2)
    side = jnp.concatenate([lse, delta], axis=1)
    side_chip = pair_rows(side, swap(side), core)
    lse_chip, delta_chip = side_chip[:, :heads], side_chip[:, heads:]
    side_half = gather_chips(side, n_out).reshape(count, 2 * heads)
    lse_half, delta_half = side_half[:, :heads], side_half[:, heads:]

    scores = jnp.einsum("qhd,khd->qhk", q_chip, k_half, preferred_element_type=jnp.float32) * scale
    probs = jnp.where(keep, jnp.exp(scores - lse_chip[:, :, None]), 0.0)
    dprob = jnp.einsum("qhd,khd->qhk", g_chip, v_half, preferred_element_type=jnp.float32)
    dscore = (probs * (dprob - delta_chip[:, :, None])).astype(jnp.bfloat16)
    q_part = jnp.einsum("qhk,khd->qhd", dscore, k_half, preferred_element_type=jnp.float32) * scale
    query_grad = merged(q_part.reshape(chip_rows, width), core).astype(jnp.bfloat16)

    scores = jnp.einsum("qhd,khd->qhk", q_half, k_chip, preferred_element_type=jnp.float32) * scale
    probs = jnp.where(keep_keys, jnp.exp(scores - lse_half[:, :, None]), 0.0)
    dprob = jnp.einsum("qhd,khd->qhk", g_half, v_chip, preferred_element_type=jnp.float32)
    dscore = (probs * (dprob - delta_half[:, :, None])).astype(jnp.bfloat16)
    key_part = jnp.einsum("qhk,qhd->khd", dscore, q_half, preferred_element_type=jnp.float32) * scale
    value_part = jnp.einsum(
        "qhk,qhd->khd", probs.astype(jnp.bfloat16), g_half, preferred_element_type=jnp.float32
    )
    kv_part = jnp.concatenate([key_part.reshape(chip_rows, width), value_part.reshape(chip_rows, width)], axis=1)
    kv_grad = merged(kv_part, core)
    key_grad = kv_grad[:, :width].astype(jnp.bfloat16)
    value_grad = kv_grad[:, width:].astype(jnp.bfloat16)
    return (mixed, query_grad, key_grad, value_grad)


def solution(mesh):
    devices = mesh.devices
    n_ctx, n_head = devices.shape
    split = Mesh(devices.reshape(n_ctx // 2, 2, n_head), ("ctxo", "core", "head"))
    rows_spec = P(CTX, "head")
    in_specs = (rows_spec, rows_spec, rows_spec, P("head", None), rows_spec, P(), P())
    out_specs = (rows_spec, rows_spec, rows_spec, rows_spec)
    return jax.shard_map(
        per_device, mesh=split, in_specs=in_specs, out_specs=out_specs, check_vma=False
    )
```

```python
import jax
import jax.numpy as jnp
from jax import lax
from jax.sharding import Mesh
from jax.sharding import PartitionSpec as P

HEAD_SIZE = 128
BLOCK = 128

NEG = -1e30
CTX = ("ctxo", "core")
SWAP = [(0, 1), (1, 0)]
GROUPS = ((0, 1), (1, 3), (3, 5))


def swap(value):
    return lax.ppermute(value, "core", SWAP)


def pair_rows(own, other, core):
    first = jnp.where(core == 0, own, other)
    second = jnp.where(core == 0, other, own)
    return jnp.concatenate([first, second], axis=0)


def halves(value, core):
    rows = value.shape[0] // 2
    top, bottom = value[:rows], value[rows:]
    own = jnp.where(core == 0, top, bottom)
    other = jnp.where(core == 0, bottom, top)
    return own, other


def per_device(queries, keys, values, out_weight, cotangent, contacts, chains):
    scale = HEAD_SIZE ** (-0.5)
    rows = queries.shape[0]
    size = HEAD_SIZE
    heads = queries.shape[1] // size
    width = heads * size
    n_out = lax.axis_size("ctxo")
    core = lax.axis_index("core")
    outer = lax.axis_index("ctxo")
    allowed = jnp.logical_or(chains[:, None] == chains[None, :], contacts > 0)
    q_blocks = rows // BLOCK
    chip_rows = 2 * rows
    count = n_out * rows

    full_cotangent = lax.all_gather(cotangent, "head", axis=1, tiled=True)
    grads = lax.dot_general(
        full_cotangent, out_weight, (((1,), (1,)), ((), ())), preferred_element_type=jnp.float32
    ).astype(jnp.bfloat16)

    q_chip = pair_rows(queries, swap(queries), core).reshape(chip_rows, heads, size)
    g_chip = pair_rows(grads, swap(grads), core).reshape(chip_rows, heads, size)
    g_own = grads.reshape(rows, heads, size)

    row_blocks = outer * (2 * q_blocks) + jnp.arange(2 * q_blocks)
    shard = 2 * jnp.arange(n_out) + core
    col_blocks = (shard[:, None] * q_blocks + jnp.arange(q_blocks)[None, :]).reshape(-1)
    part_mask = allowed[row_blocks][:, col_blocks]
    keep = jnp.repeat(jnp.repeat(part_mask, BLOCK, axis=0), BLOCK, axis=1)[:, None, :]

    pair = jnp.stack([keys, values])
    spread = jnp.broadcast_to(pair[None], (n_out,) + pair.shape)
    gathered = lax.all_to_all(spread, "ctxo", 0, 0, tiled=True)
    k_all = gathered[:, 0].reshape(count, heads, size)
    v_all = gathered[:, 1].reshape(count, heads, size)

    scores = jnp.einsum("qhd,khd->qhk", q_chip, k_all, preferred_element_type=jnp.float32) * scale
    scores = jnp.where(keep, scores, NEG)
    best = jnp.max(scores, axis=2)
    weights = jnp.where(keep, jnp.exp(scores - best[:, :, None]), 0.0)
    total = jnp.sum(weights, axis=2)
    accum = jnp.einsum(
        "qhk,khd->qhd", weights.astype(jnp.bfloat16), v_all, preferred_element_type=jnp.float32
    )

    state = jnp.concatenate([best, total, accum.reshape(chip_rows, width)], axis=1)
    own_state, other_state = halves(state, core)
    got_state = swap(other_state)
    best_a, total_a, acc_a = own_state[:, :heads], own_state[:, heads:2 * heads], own_state[:, 2 * heads:]
    best_b, total_b, acc_b = got_state[:, :heads], got_state[:, heads:2 * heads], got_state[:, 2 * heads:]
    best_m = jnp.maximum(best_a, best_b)
    fa = jnp.exp(best_a - best_m)
    fb = jnp.exp(best_b - best_m)
    total_m = total_a * fa + total_b * fb
    acc_m = acc_a.reshape(rows, heads, size) * fa[:, :, None] + acc_b.reshape(rows, heads, size) * fb[:, :, None]
    attended = (acc_m / total_m[:, :, None]).astype(jnp.bfloat16)
    lse_all = best_m + jnp.log(total_m)
    attended_parts = [attended[:, lo:hi] for lo, hi in GROUPS]
    lse_parts = [lse_all[:, lo:hi] for lo, hi in GROUPS]
    kv_parts = [(k_all[:, lo:hi], v_all[:, lo:hi]) for lo, hi in GROUPS]

    projected = jnp.dot(attended.reshape(rows, width), out_weight, preferred_element_type=jnp.float32)
    mixed = lax.psum_scatter(projected.astype(jnp.bfloat16), "head", scatter_dimension=1, tiled=True)

    q_grads, k_grads, v_grads = [], [], []
    for (lo, hi), att, lse, (k_three, v_three) in zip(GROUPS, attended_parts, lse_parts, kv_parts):
        span = hi - lo
        q_three = q_chip[:, lo:hi]
        g_three = g_chip[:, lo:hi]
        delta = jnp.sum(g_own[:, lo:hi].astype(jnp.float32) * att.astype(jnp.float32), axis=2)
        side = jnp.concatenate([lse, delta], axis=1)
        side_chip = pair_rows(side, swap(side), core)
        lse_chip, delta_chip = side_chip[:, :span], side_chip[:, span:]

        scores = jnp.einsum("qhd,khd->qhk", q_three, k_three, preferred_element_type=jnp.float32) * scale
        probs = jnp.where(keep, jnp.exp(scores - lse_chip[:, :, None]), 0.0)
        dprob = jnp.einsum("qhd,khd->qhk", g_three, v_three, preferred_element_type=jnp.float32)
        dscore = (probs * (dprob - delta_chip[:, :, None])).astype(jnp.bfloat16)

        q_part = jnp.einsum("qhk,khd->qhd", dscore, k_three, preferred_element_type=jnp.float32) * scale
        q_own, q_other = halves(q_part.reshape(chip_rows, span * size), core)
        q_grads.append((q_own + swap(q_other)).astype(jnp.bfloat16))

        key_part = (
            jnp.einsum("qhk,qhd->khd", dscore, q_three, preferred_element_type=jnp.float32) * scale
        ).astype(jnp.bfloat16)
        value_part = jnp.einsum(
            "qhk,qhd->khd", probs.astype(jnp.bfloat16), g_three, preferred_element_type=jnp.float32
        ).astype(jnp.bfloat16)
        grad_parts = jnp.stack(
            [key_part.reshape(n_out, rows, span * size), value_part.reshape(n_out, rows, span * size)],
            axis=1,
        )
        summed = jnp.sum(
            lax.all_to_all(grad_parts, "ctxo", 0, 0, tiled=True).astype(jnp.float32), axis=0
        )
        k_grads.append(summed[0].astype(jnp.bfloat16))
        v_grads.append(summed[1].astype(jnp.bfloat16))

    query_grad = jnp.concatenate(q_grads, axis=1)
    key_grad = jnp.concatenate(k_grads, axis=1)
    value_grad = jnp.concatenate(v_grads, axis=1)
    return (mixed, query_grad, key_grad, value_grad)


def solution(mesh):
    devices = mesh.devices
    n_ctx, n_head = devices.shape
    split = Mesh(devices.reshape(n_ctx // 2, 2, n_head), ("ctxo", "core", "head"))
    rows_spec = P(CTX, "head")
    in_specs = (rows_spec, rows_spec, rows_spec, P("head", None), rows_spec, P(), P())
    out_specs = (rows_spec, rows_spec, rows_spec, rows_spec)
    return jax.shard_map(
        per_device, mesh=split, in_specs=in_specs, out_specs=out_specs, check_vma=False
    )
```

```python
import jax
import jax.numpy as jnp
from jax import lax
from jax.sharding import Mesh
from jax.sharding import PartitionSpec as P

HEAD_SIZE = 128
BLOCK = 128

NEG = -1e30
CTX = ("ctxo", "core")
SWAP = [(0, 1), (1, 0)]
GROUPS = ((0, 1), (1, 3), (3, 5))


def swap(value):
    return lax.ppermute(value, "core", SWAP)


def pair_rows(own, other, core):
    first = jnp.where(core == 0, own, other)
    second = jnp.where(core == 0, other, own)
    return jnp.concatenate([first, second], axis=0)


def halves(value, core):
    rows = value.shape[0] // 2
    top, bottom = value[:rows], value[rows:]
    own = jnp.where(core == 0, top, bottom)
    other = jnp.where(core == 0, bottom, top)
    return own, other


def per_device(queries, keys, values, out_weight, cotangent, contacts, chains):
    scale = HEAD_SIZE ** (-0.5)
    rows = queries.shape[0]
    size = HEAD_SIZE
    heads = queries.shape[1] // size
    width = heads * size
    n_out = lax.axis_size("ctxo")
    core = lax.axis_index("core")
    outer = lax.axis_index("ctxo")
    allowed = jnp.logical_or(chains[:, None] == chains[None, :], contacts > 0)
    q_blocks = rows // BLOCK
    chip_rows = 2 * rows
    count = n_out * rows

    full_cotangent = lax.all_gather(cotangent, "head", axis=1, tiled=True)
    grads = lax.dot_general(
        full_cotangent, out_weight, (((1,), (1,)), ((), ())), preferred_element_type=jnp.float32
    ).astype(jnp.bfloat16)

    q_chip = pair_rows(queries, swap(queries), core).reshape(chip_rows, heads, size)
    g_chip = pair_rows(grads, swap(grads), core).reshape(chip_rows, heads, size)
    g_own = grads.reshape(rows, heads, size)

    row_blocks = outer * (2 * q_blocks) + jnp.arange(2 * q_blocks)
    shard = 2 * jnp.arange(n_out) + core
    col_blocks = (shard[:, None] * q_blocks + jnp.arange(q_blocks)[None, :]).reshape(-1)
    part_mask = allowed[row_blocks][:, col_blocks]
    keep = jnp.repeat(jnp.repeat(part_mask, BLOCK, axis=0), BLOCK, axis=1)[:, None, :]

    attended_parts, lse_parts, kv_parts = [], [], []
    for lo, hi in GROUPS:
        span = hi - lo
        cols = slice(lo * size, hi * size)
        pair = jnp.stack([keys[:, cols], values[:, cols]])
        spread = jnp.broadcast_to(pair[None], (n_out,) + pair.shape)
        if len(attended_parts) > 1:
            spread, _ = lax.optimization_barrier((spread, attended_parts[-2]))
        gathered = lax.all_to_all(spread, "ctxo", 0, 0, tiled=True)
        k_three = gathered[:, 0].reshape(count, span, size)
        v_three = gathered[:, 1].reshape(count, span, size)
        kv_parts.append((k_three, v_three))
        q_three = q_chip[:, lo:hi]

        scores = jnp.einsum("qhd,khd->qhk", q_three, k_three, preferred_element_type=jnp.float32) * scale
        scores = jnp.where(keep, scores, NEG)
        best = jnp.max(scores, axis=2)
        weights = jnp.where(keep, jnp.exp(scores - best[:, :, None]), 0.0)
        total = jnp.sum(weights, axis=2)
        accum = jnp.einsum(
            "qhk,khd->qhd", weights.astype(jnp.bfloat16), v_three, preferred_element_type=jnp.float32
        )

        state = jnp.concatenate([best, total, accum.reshape(chip_rows, span * size)], axis=1)
        own_state, other_state = halves(state, core)
        got_state = swap(other_state)
        best_a, total_a, acc_a = own_state[:, :span], own_state[:, span:2 * span], own_state[:, 2 * span:]
        best_b, total_b, acc_b = got_state[:, :span], got_state[:, span:2 * span], got_state[:, 2 * span:]
        best_m = jnp.maximum(best_a, best_b)
        fa = jnp.exp(best_a - best_m)
        fb = jnp.exp(best_b - best_m)
        total_m = total_a * fa + total_b * fb
        acc_m = (
            acc_a.reshape(rows, span, size) * fa[:, :, None]
            + acc_b.reshape(rows, span, size) * fb[:, :, None]
        )
        attended_parts.append((acc_m / total_m[:, :, None]).astype(jnp.bfloat16))
        lse_parts.append(best_m + jnp.log(total_m))

    attended = jnp.concatenate(attended_parts, axis=1)

    projected = jnp.dot(attended.reshape(rows, width), out_weight, preferred_element_type=jnp.float32)
    mixed = lax.psum_scatter(projected.astype(jnp.bfloat16), "head", scatter_dimension=1, tiled=True)

    q_grads, k_grads, v_grads = [], [], []
    for (lo, hi), att, lse, (k_three, v_three) in zip(GROUPS, attended_parts, lse_parts, kv_parts):
        span = hi - lo
        q_three = q_chip[:, lo:hi]
        g_three = g_chip[:, lo:hi]
        delta = jnp.sum(g_own[:, lo:hi].astype(jnp.float32) * att.astype(jnp.float32), axis=2)
        side = jnp.concatenate([lse, delta], axis=1)
        side_chip = pair_rows(side, swap(side), core)
        lse_chip, delta_chip = side_chip[:, :span], side_chip[:, span:]

        scores = jnp.einsum("qhd,khd->qhk", q_three, k_three, preferred_element_type=jnp.float32) * scale
        probs = jnp.where(keep, jnp.exp(scores - lse_chip[:, :, None]), 0.0)
        dprob = jnp.einsum("qhd,khd->qhk", g_three, v_three, preferred_element_type=jnp.float32)
        dscore = (probs * (dprob - delta_chip[:, :, None])).astype(jnp.bfloat16)

        q_part = jnp.einsum("qhk,khd->qhd", dscore, k_three, preferred_element_type=jnp.float32) * scale
        q_own, q_other = halves(q_part.reshape(chip_rows, span * size), core)
        q_grads.append((q_own + swap(q_other)).astype(jnp.bfloat16))

        key_part = (
            jnp.einsum("qhk,qhd->khd", dscore, q_three, preferred_element_type=jnp.float32) * scale
        ).astype(jnp.bfloat16)
        value_part = jnp.einsum(
            "qhk,qhd->khd", probs.astype(jnp.bfloat16), g_three, preferred_element_type=jnp.float32
        ).astype(jnp.bfloat16)
        grad_parts = jnp.stack(
            [key_part.reshape(n_out, rows, span * size), value_part.reshape(n_out, rows, span * size)],
            axis=1,
        )
        summed = jnp.sum(
            lax.all_to_all(grad_parts, "ctxo", 0, 0, tiled=True).astype(jnp.float32), axis=0
        )
        k_grads.append(summed[0].astype(jnp.bfloat16))
        v_grads.append(summed[1].astype(jnp.bfloat16))

    query_grad = jnp.concatenate(q_grads, axis=1)
    key_grad = jnp.concatenate(k_grads, axis=1)
    value_grad = jnp.concatenate(v_grads, axis=1)
    return (mixed, query_grad, key_grad, value_grad)


def solution(mesh):
    devices = mesh.devices
    n_ctx, n_head = devices.shape
    split = Mesh(devices.reshape(n_ctx // 2, 2, n_head), ("ctxo", "core", "head"))
    rows_spec = P(CTX, "head")
    in_specs = (rows_spec, rows_spec, rows_spec, P("head", None), rows_spec, P(), P())
    out_specs = (rows_spec, rows_spec, rows_spec, rows_spec)
    return jax.shard_map(
        per_device, mesh=split, in_specs=in_specs, out_specs=out_specs, check_vma=False
    )
```

```python
import jax
import jax.numpy as jnp
from jax import lax
from jax.sharding import Mesh
from jax.sharding import PartitionSpec as P

HEAD_SIZE = 128
BLOCK = 128

NEG = -1e30
CTX = ("ctxo", "core")
SWAP = [(0, 1), (1, 0)]
GROUPS = ((0, 1), (1, 2), (2, 3), (3, 4), (4, 5))


def swap(value):
    return lax.ppermute(value, "core", SWAP)


def pair_rows(own, other, core):
    first = jnp.where(core == 0, own, other)
    second = jnp.where(core == 0, other, own)
    return jnp.concatenate([first, second], axis=0)


def halves(value, core):
    rows = value.shape[0] // 2
    top, bottom = value[:rows], value[rows:]
    own = jnp.where(core == 0, top, bottom)
    other = jnp.where(core == 0, bottom, top)
    return own, other


def per_device(queries, keys, values, out_weight, cotangent, contacts, chains):
    scale = HEAD_SIZE ** (-0.5)
    rows = queries.shape[0]
    size = HEAD_SIZE
    heads = queries.shape[1] // size
    width = heads * size
    n_out = lax.axis_size("ctxo")
    core = lax.axis_index("core")
    outer = lax.axis_index("ctxo")
    allowed = jnp.logical_or(chains[:, None] == chains[None, :], contacts > 0)
    q_blocks = rows // BLOCK
    chip_rows = 2 * rows
    count = n_out * rows

    full_cotangent = lax.all_gather(cotangent, "head", axis=1, tiled=True)
    grads = lax.dot_general(
        full_cotangent, out_weight, (((1,), (1,)), ((), ())), preferred_element_type=jnp.float32
    ).astype(jnp.bfloat16)

    q_chip = pair_rows(queries, swap(queries), core).reshape(chip_rows, heads, size)
    g_chip = pair_rows(grads, swap(grads), core).reshape(chip_rows, heads, size)
    g_own = grads.reshape(rows, heads, size)

    row_blocks = outer * (2 * q_blocks) + jnp.arange(2 * q_blocks)
    shard = 2 * jnp.arange(n_out) + core
    col_blocks = (shard[:, None] * q_blocks + jnp.arange(q_blocks)[None, :]).reshape(-1)
    part_mask = allowed[row_blocks][:, col_blocks]
    keep = jnp.repeat(jnp.repeat(part_mask, BLOCK, axis=0), BLOCK, axis=1)[:, None, :]

    attended_parts, lse_parts, kv_parts = [], [], []
    for lo, hi in GROUPS:
        span = hi - lo
        cols = slice(lo * size, hi * size)
        pair = jnp.stack([keys[:, cols], values[:, cols]])
        spread = jnp.broadcast_to(pair[None], (n_out,) + pair.shape)
        gathered = lax.all_to_all(spread, "ctxo", 0, 0, tiled=True)
        k_three = gathered[:, 0].reshape(count, span, size)
        v_three = gathered[:, 1].reshape(count, span, size)
        kv_parts.append((k_three, v_three))
        q_three = q_chip[:, lo:hi]

        scores = jnp.einsum("qhd,khd->qhk", q_three, k_three, preferred_element_type=jnp.float32) * scale
        scores = jnp.where(keep, scores, NEG)
        best = jnp.max(scores, axis=2)
        weights = jnp.where(keep, jnp.exp(scores - best[:, :, None]), 0.0)
        total = jnp.sum(weights, axis=2)
        accum = jnp.einsum(
            "qhk,khd->qhd", weights.astype(jnp.bfloat16), v_three, preferred_element_type=jnp.float32
        )

        state = jnp.concatenate([best, total, accum.reshape(chip_rows, span * size)], axis=1)
        own_state, other_state = halves(state, core)
        got_state = swap(other_state)
        best_a, total_a, acc_a = own_state[:, :span], own_state[:, span:2 * span], own_state[:, 2 * span:]
        best_b, total_b, acc_b = got_state[:, :span], got_state[:, span:2 * span], got_state[:, 2 * span:]
        best_m = jnp.maximum(best_a, best_b)
        fa = jnp.exp(best_a - best_m)
        fb = jnp.exp(best_b - best_m)
        total_m = total_a * fa + total_b * fb
        acc_m = (
            acc_a.reshape(rows, span, size) * fa[:, :, None]
            + acc_b.reshape(rows, span, size) * fb[:, :, None]
        )
        attended_parts.append((acc_m / total_m[:, :, None]).astype(jnp.bfloat16))
        lse_parts.append(best_m + jnp.log(total_m))

    attended = jnp.concatenate(attended_parts, axis=1)

    projected = jnp.dot(attended.reshape(rows, width), out_weight, preferred_element_type=jnp.float32)
    mixed = lax.psum_scatter(projected.astype(jnp.bfloat16), "head", scatter_dimension=1, tiled=True)

    q_grads, k_grads, v_grads = [], [], []
    for (lo, hi), att, lse, (k_three, v_three) in zip(GROUPS, attended_parts, lse_parts, kv_parts):
        span = hi - lo
        q_three = q_chip[:, lo:hi]
        g_three = g_chip[:, lo:hi]
        delta = jnp.sum(g_own[:, lo:hi].astype(jnp.float32) * att.astype(jnp.float32), axis=2)
        side = jnp.concatenate([lse, delta], axis=1)
        side_chip = pair_rows(side, swap(side), core)
        lse_chip, delta_chip = side_chip[:, :span], side_chip[:, span:]

        scores = jnp.einsum("qhd,khd->qhk", q_three, k_three, preferred_element_type=jnp.float32) * scale
        probs = jnp.where(keep, jnp.exp(scores - lse_chip[:, :, None]), 0.0)
        dprob = jnp.einsum("qhd,khd->qhk", g_three, v_three, preferred_element_type=jnp.float32)
        dscore = (probs * (dprob - delta_chip[:, :, None])).astype(jnp.bfloat16)

        q_part = jnp.einsum("qhk,khd->qhd", dscore, k_three, preferred_element_type=jnp.float32) * scale
        q_own, q_other = halves(q_part.reshape(chip_rows, span * size), core)
        q_grads.append((q_own + swap(q_other)).astype(jnp.bfloat16))

        key_part = (
            jnp.einsum("qhk,qhd->khd", dscore, q_three, preferred_element_type=jnp.float32) * scale
        ).astype(jnp.bfloat16)
        value_part = jnp.einsum(
            "qhk,qhd->khd", probs.astype(jnp.bfloat16), g_three, preferred_element_type=jnp.float32
        ).astype(jnp.bfloat16)
        grad_parts = jnp.stack(
            [key_part.reshape(n_out, rows, span * size), value_part.reshape(n_out, rows, span * size)],
            axis=1,
        )
        summed = jnp.sum(
            lax.all_to_all(grad_parts, "ctxo", 0, 0, tiled=True).astype(jnp.float32), axis=0
        )
        k_grads.append(summed[0].astype(jnp.bfloat16))
        v_grads.append(summed[1].astype(jnp.bfloat16))

    query_grad = jnp.concatenate(q_grads, axis=1)
    key_grad = jnp.concatenate(k_grads, axis=1)
    value_grad = jnp.concatenate(v_grads, axis=1)
    return (mixed, query_grad, key_grad, value_grad)


def solution(mesh):
    devices = mesh.devices
    n_ctx, n_head = devices.shape
    split = Mesh(devices.reshape(n_ctx // 2, 2, n_head), ("ctxo", "core", "head"))
    rows_spec = P(CTX, "head")
    in_specs = (rows_spec, rows_spec, rows_spec, P("head", None), rows_spec, P(), P())
    out_specs = (rows_spec, rows_spec, rows_spec, rows_spec)
    return jax.shard_map(
        per_device, mesh=split, in_specs=in_specs, out_specs=out_specs, check_vma=False
    )
```

```python
import jax
import jax.numpy as jnp
from jax import lax
from jax.sharding import Mesh
from jax.sharding import PartitionSpec as P

HEAD_SIZE = 128
BLOCK = 128

NEG = -1e30
CTX = ("ctxo", "core")
SWAP = [(0, 1), (1, 0)]
GROUPS = ((0, 2), (2, 5))


def swap(value):
    return lax.ppermute(value, "core", SWAP)


def pair_rows(own, other, core):
    first = jnp.where(core == 0, own, other)
    second = jnp.where(core == 0, other, own)
    return jnp.concatenate([first, second], axis=0)


def halves(value, core):
    rows = value.shape[0] // 2
    top, bottom = value[:rows], value[rows:]
    own = jnp.where(core == 0, top, bottom)
    other = jnp.where(core == 0, bottom, top)
    return own, other


def per_device(queries, keys, values, out_weight, cotangent, contacts, chains):
    scale = HEAD_SIZE ** (-0.5)
    rows = queries.shape[0]
    size = HEAD_SIZE
    heads = queries.shape[1] // size
    width = heads * size
    n_out = lax.axis_size("ctxo")
    core = lax.axis_index("core")
    outer = lax.axis_index("ctxo")
    allowed = jnp.logical_or(chains[:, None] == chains[None, :], contacts > 0)
    q_blocks = rows // BLOCK
    chip_rows = 2 * rows
    count = n_out * rows

    full_cotangent = lax.all_gather(cotangent, "head", axis=1, tiled=True)
    grads = lax.dot_general(
        full_cotangent, out_weight, (((1,), (1,)), ((), ())), preferred_element_type=jnp.float32
    ).astype(jnp.bfloat16)

    q_chip = pair_rows(queries, swap(queries), core).reshape(chip_rows, heads, size)
    g_chip = pair_rows(grads, swap(grads), core).reshape(chip_rows, heads, size)
    g_own = grads.reshape(rows, heads, size)

    row_blocks = outer * (2 * q_blocks) + jnp.arange(2 * q_blocks)
    shard = 2 * jnp.arange(n_out) + core
    col_blocks = (shard[:, None] * q_blocks + jnp.arange(q_blocks)[None, :]).reshape(-1)
    part_mask = allowed[row_blocks][:, col_blocks]
    keep = jnp.repeat(jnp.repeat(part_mask, BLOCK, axis=0), BLOCK, axis=1)[:, None, :]

    attended_parts, lse_parts, kv_parts = [], [], []
    for lo, hi in GROUPS:
        span = hi - lo
        cols = slice(lo * size, hi * size)
        pair = jnp.stack([keys[:, cols], values[:, cols]])
        spread = jnp.broadcast_to(pair[None], (n_out,) + pair.shape)
        gathered = lax.all_to_all(spread, "ctxo", 0, 0, tiled=True)
        k_three = gathered[:, 0].reshape(count, span, size)
        v_three = gathered[:, 1].reshape(count, span, size)
        kv_parts.append((k_three, v_three))
        q_three = q_chip[:, lo:hi]

        scores = jnp.einsum("qhd,khd->qhk", q_three, k_three, preferred_element_type=jnp.float32) * scale
        scores = jnp.where(keep, scores, NEG)
        best = jnp.max(scores, axis=2)
        weights = jnp.where(keep, jnp.exp(scores - best[:, :, None]), 0.0)
        total = jnp.sum(weights, axis=2)
        accum = jnp.einsum(
            "qhk,khd->qhd", weights.astype(jnp.bfloat16), v_three, preferred_element_type=jnp.float32
        )

        state = jnp.concatenate([best, total, accum.reshape(chip_rows, span * size)], axis=1)
        own_state, other_state = halves(state, core)
        got_state = swap(other_state)
        best_a, total_a, acc_a = own_state[:, :span], own_state[:, span:2 * span], own_state[:, 2 * span:]
        best_b, total_b, acc_b = got_state[:, :span], got_state[:, span:2 * span], got_state[:, 2 * span:]
        best_m = jnp.maximum(best_a, best_b)
        fa = jnp.exp(best_a - best_m)
        fb = jnp.exp(best_b - best_m)
        total_m = total_a * fa + total_b * fb
        acc_m = (
            acc_a.reshape(rows, span, size) * fa[:, :, None]
            + acc_b.reshape(rows, span, size) * fb[:, :, None]
        )
        attended_parts.append((acc_m / total_m[:, :, None]).astype(jnp.bfloat16))
        lse_parts.append(best_m + jnp.log(total_m))

    attended = jnp.concatenate(attended_parts, axis=1)

    projected = jnp.dot(attended.reshape(rows, width), out_weight, preferred_element_type=jnp.float32)
    mixed = lax.psum_scatter(projected.astype(jnp.bfloat16), "head", scatter_dimension=1, tiled=True)

    q_grads, k_grads, v_grads = [], [], []
    for (lo, hi), att, lse, (k_three, v_three) in zip(GROUPS, attended_parts, lse_parts, kv_parts):
        span = hi - lo
        q_three = q_chip[:, lo:hi]
        g_three = g_chip[:, lo:hi]
        delta = jnp.sum(g_own[:, lo:hi].astype(jnp.float32) * att.astype(jnp.float32), axis=2)
        side = jnp.concatenate([lse, delta], axis=1)
        side_chip = pair_rows(side, swap(side), core)
        lse_chip, delta_chip = side_chip[:, :span], side_chip[:, span:]

        scores = jnp.einsum("qhd,khd->qhk", q_three, k_three, preferred_element_type=jnp.float32) * scale
        probs = jnp.where(keep, jnp.exp(scores - lse_chip[:, :, None]), 0.0)
        dprob = jnp.einsum("qhd,khd->qhk", g_three, v_three, preferred_element_type=jnp.float32)
        dscore = (probs * (dprob - delta_chip[:, :, None])).astype(jnp.bfloat16)

        q_part = jnp.einsum("qhk,khd->qhd", dscore, k_three, preferred_element_type=jnp.float32) * scale
        q_own, q_other = halves(q_part.reshape(chip_rows, span * size), core)
        q_grads.append((q_own + swap(q_other)).astype(jnp.bfloat16))

        key_part = (
            jnp.einsum("qhk,qhd->khd", dscore, q_three, preferred_element_type=jnp.float32) * scale
        ).astype(jnp.bfloat16)
        value_part = jnp.einsum(
            "qhk,qhd->khd", probs.astype(jnp.bfloat16), g_three, preferred_element_type=jnp.float32
        ).astype(jnp.bfloat16)
        grad_parts = jnp.stack(
            [key_part.reshape(n_out, rows, span * size), value_part.reshape(n_out, rows, span * size)],
            axis=1,
        )
        summed = jnp.sum(
            lax.all_to_all(grad_parts, "ctxo", 0, 0, tiled=True).astype(jnp.float32), axis=0
        )
        k_grads.append(summed[0].astype(jnp.bfloat16))
        v_grads.append(summed[1].astype(jnp.bfloat16))

    query_grad = jnp.concatenate(q_grads, axis=1)
    key_grad = jnp.concatenate(k_grads, axis=1)
    value_grad = jnp.concatenate(v_grads, axis=1)
    return (mixed, query_grad, key_grad, value_grad)


def solution(mesh):
    devices = mesh.devices
    n_ctx, n_head = devices.shape
    split = Mesh(devices.reshape(n_ctx // 2, 2, n_head), ("ctxo", "core", "head"))
    rows_spec = P(CTX, "head")
    in_specs = (rows_spec, rows_spec, rows_spec, P("head", None), rows_spec, P(), P())
    out_specs = (rows_spec, rows_spec, rows_spec, rows_spec)
    return jax.shard_map(
        per_device, mesh=split, in_specs=in_specs, out_specs=out_specs, check_vma=False
    )
```

```python
import jax
import jax.numpy as jnp
from jax import lax
from jax.sharding import Mesh
from jax.sharding import PartitionSpec as P

HEAD_SIZE = 128
BLOCK = 128

NEG = -1e30
CTX = ("ctxo", "core")
SWAP = [(0, 1), (1, 0)]
GROUPS = ((0, 1), (1, 3), (3, 5))


def swap(value):
    return lax.ppermute(value, "core", SWAP)


def pair_rows(own, other, core):
    first = jnp.where(core == 0, own, other)
    second = jnp.where(core == 0, other, own)
    return jnp.concatenate([first, second], axis=0)


def halves(value, core):
    rows = value.shape[0] // 2
    top, bottom = value[:rows], value[rows:]
    own = jnp.where(core == 0, top, bottom)
    other = jnp.where(core == 0, bottom, top)
    return own, other


def per_device(queries, keys, values, out_weight, cotangent, contacts, chains):
    scale = HEAD_SIZE ** (-0.5)
    rows = queries.shape[0]
    size = HEAD_SIZE
    heads = queries.shape[1] // size
    width = heads * size
    n_out = lax.axis_size("ctxo")
    core = lax.axis_index("core")
    outer = lax.axis_index("ctxo")
    allowed = jnp.logical_or(chains[:, None] == chains[None, :], contacts > 0)
    q_blocks = rows // BLOCK
    chip_rows = 2 * rows
    count = n_out * rows

    full_cotangent = lax.all_gather(cotangent, "head", axis=1, tiled=True)
    grads = lax.dot_general(
        full_cotangent, out_weight, (((1,), (1,)), ((), ())), preferred_element_type=jnp.float32
    ).astype(jnp.bfloat16)

    q_chip = pair_rows(queries, swap(queries), core).reshape(chip_rows, heads, size)
    g_chip = pair_rows(grads, swap(grads), core).reshape(chip_rows, heads, size)
    g_own = grads.reshape(rows, heads, size)

    row_blocks = outer * (2 * q_blocks) + jnp.arange(2 * q_blocks)
    shard = 2 * jnp.arange(n_out) + core
    col_blocks = (shard[:, None] * q_blocks + jnp.arange(q_blocks)[None, :]).reshape(-1)
    part_mask = allowed[row_blocks][:, col_blocks]
    keep = jnp.repeat(jnp.repeat(part_mask, BLOCK, axis=0), BLOCK, axis=1)[:, None, :]

    attended_parts, lse_parts, kv_parts = [], [], []
    for lo, hi in GROUPS:
        span = hi - lo
        cols = slice(lo * size, hi * size)
        pair = jnp.stack([keys[:, cols], values[:, cols]])
        spread = jnp.broadcast_to(pair[None], (n_out,) + pair.shape)
        gathered = lax.all_to_all(spread, "ctxo", 0, 0, tiled=True)
        if attended_parts:
            gathered, _ = lax.optimization_barrier((gathered, attended_parts[-1]))
        k_three = gathered[:, 0].reshape(count, span, size)
        v_three = gathered[:, 1].reshape(count, span, size)
        kv_parts.append((k_three, v_three))
        q_three = q_chip[:, lo:hi]

        scores = jnp.einsum("qhd,khd->qhk", q_three, k_three, preferred_element_type=jnp.float32) * scale
        scores = jnp.where(keep, scores, NEG)
        best = jnp.max(scores, axis=2)
        weights = jnp.where(keep, jnp.exp(scores - best[:, :, None]), 0.0)
        total = jnp.sum(weights, axis=2)
        accum = jnp.einsum(
            "qhk,khd->qhd", weights.astype(jnp.bfloat16), v_three, preferred_element_type=jnp.float32
        )

        state = jnp.concatenate([best, total, accum.reshape(chip_rows, span * size)], axis=1)
        own_state, other_state = halves(state, core)
        got_state = swap(other_state)
        best_a, total_a, acc_a = own_state[:, :span], own_state[:, span:2 * span], own_state[:, 2 * span:]
        best_b, total_b, acc_b = got_state[:, :span], got_state[:, span:2 * span], got_state[:, 2 * span:]
        best_m = jnp.maximum(best_a, best_b)
        fa = jnp.exp(best_a - best_m)
        fb = jnp.exp(best_b - best_m)
        total_m = total_a * fa + total_b * fb
        acc_m = (
            acc_a.reshape(rows, span, size) * fa[:, :, None]
            + acc_b.reshape(rows, span, size) * fb[:, :, None]
        )
        attended_parts.append((acc_m / total_m[:, :, None]).astype(jnp.bfloat16))
        lse_parts.append(best_m + jnp.log(total_m))

    attended = jnp.concatenate(attended_parts, axis=1)

    projected = jnp.dot(attended.reshape(rows, width), out_weight, preferred_element_type=jnp.float32)
    mixed = lax.psum_scatter(projected.astype(jnp.bfloat16), "head", scatter_dimension=1, tiled=True)

    q_grads, k_grads, v_grads = [], [], []
    for (lo, hi), att, lse, (k_three, v_three) in zip(GROUPS, attended_parts, lse_parts, kv_parts):
        span = hi - lo
        q_three = q_chip[:, lo:hi]
        g_three = g_chip[:, lo:hi]
        delta = jnp.sum(g_own[:, lo:hi].astype(jnp.float32) * att.astype(jnp.float32), axis=2)
        side = jnp.concatenate([lse, delta], axis=1)
        side_chip = pair_rows(side, swap(side), core)
        lse_chip, delta_chip = side_chip[:, :span], side_chip[:, span:]

        scores = jnp.einsum("qhd,khd->qhk", q_three, k_three, preferred_element_type=jnp.float32) * scale
        probs = jnp.where(keep, jnp.exp(scores - lse_chip[:, :, None]), 0.0)
        dprob = jnp.einsum("qhd,khd->qhk", g_three, v_three, preferred_element_type=jnp.float32)
        dscore = (probs * (dprob - delta_chip[:, :, None])).astype(jnp.bfloat16)

        q_part = jnp.einsum("qhk,khd->qhd", dscore, k_three, preferred_element_type=jnp.float32) * scale
        q_own, q_other = halves(q_part.reshape(chip_rows, span * size), core)
        q_grads.append((q_own + swap(q_other)).astype(jnp.bfloat16))

        key_part = (
            jnp.einsum("qhk,qhd->khd", dscore, q_three, preferred_element_type=jnp.float32) * scale
        ).astype(jnp.bfloat16)
        value_part = jnp.einsum(
            "qhk,qhd->khd", probs.astype(jnp.bfloat16), g_three, preferred_element_type=jnp.float32
        ).astype(jnp.bfloat16)
        grad_parts = jnp.stack(
            [key_part.reshape(n_out, rows, span * size), value_part.reshape(n_out, rows, span * size)],
            axis=1,
        )
        summed = jnp.sum(
            lax.all_to_all(grad_parts, "ctxo", 0, 0, tiled=True).astype(jnp.float32), axis=0
        )
        k_grads.append(summed[0].astype(jnp.bfloat16))
        v_grads.append(summed[1].astype(jnp.bfloat16))

    query_grad = jnp.concatenate(q_grads, axis=1)
    key_grad = jnp.concatenate(k_grads, axis=1)
    value_grad = jnp.concatenate(v_grads, axis=1)
    return (mixed, query_grad, key_grad, value_grad)


def solution(mesh):
    devices = mesh.devices
    n_ctx, n_head = devices.shape
    split = Mesh(devices.reshape(n_ctx // 2, 2, n_head), ("ctxo", "core", "head"))
    rows_spec = P(CTX, "head")
    in_specs = (rows_spec, rows_spec, rows_spec, P("head", None), rows_spec, P(), P())
    out_specs = (rows_spec, rows_spec, rows_spec, rows_spec)
    return jax.shard_map(
        per_device, mesh=split, in_specs=in_specs, out_specs=out_specs, check_vma=False
    )
```

```python
import jax
import jax.numpy as jnp
from jax import lax
from jax.sharding import Mesh
from jax.sharding import PartitionSpec as P

HEAD_SIZE = 128
BLOCK = 128

NEG = -1e30
CTX = ("ctxo", "core")
SWAP = [(0, 1), (1, 0)]
GROUPS = ((0, 1), (1, 3), (3, 5))


def swap(value):
    return lax.ppermute(value, "core", SWAP)


def pair_rows(own, other, core):
    first = jnp.where(core == 0, own, other)
    second = jnp.where(core == 0, other, own)
    return jnp.concatenate([first, second], axis=0)


def halves(value, core):
    rows = value.shape[0] // 2
    top, bottom = value[:rows], value[rows:]
    own = jnp.where(core == 0, top, bottom)
    other = jnp.where(core == 0, bottom, top)
    return own, other


def per_device(queries, keys, values, out_weight, cotangent, contacts, chains):
    scale = HEAD_SIZE ** (-0.5)
    rows = queries.shape[0]
    size = HEAD_SIZE
    heads = queries.shape[1] // size
    width = heads * size
    n_out = lax.axis_size("ctxo")
    core = lax.axis_index("core")
    outer = lax.axis_index("ctxo")
    allowed = jnp.logical_or(chains[:, None] == chains[None, :], contacts > 0)
    q_blocks = rows // BLOCK
    chip_rows = 2 * rows
    count = n_out * rows

    full_cotangent = lax.all_gather(cotangent, "head", axis=1, tiled=True)
    grads = lax.dot_general(
        full_cotangent, out_weight, (((1,), (1,)), ((), ())), preferred_element_type=jnp.float32
    ).astype(jnp.bfloat16)

    q_chip = pair_rows(queries, swap(queries), core).reshape(chip_rows, heads, size)
    g_chip = pair_rows(grads, swap(grads), core).reshape(chip_rows, heads, size)
    g_own = grads.reshape(rows, heads, size)

    row_blocks = outer * (2 * q_blocks) + jnp.arange(2 * q_blocks)
    shard = 2 * jnp.arange(n_out) + core
    col_blocks = (shard[:, None] * q_blocks + jnp.arange(q_blocks)[None, :]).reshape(-1)
    part_mask = allowed[row_blocks][:, col_blocks]
    keep = jnp.repeat(jnp.repeat(part_mask, BLOCK, axis=0), BLOCK, axis=1)[:, None, :]

    attended_parts, lse_parts, kv_parts = [], [], []
    for lo, hi in GROUPS:
        span = hi - lo
        cols = slice(lo * size, hi * size)
        pair = jnp.stack([keys[:, cols], values[:, cols]])
        spread = jnp.broadcast_to(pair[None], (n_out,) + pair.shape)
        gathered = lax.all_to_all(spread, "ctxo", 0, 0, tiled=True)
        k_three = gathered[:, 0].reshape(count, span, size)
        v_three = gathered[:, 1].reshape(count, span, size)
        kv_parts.append((k_three, v_three))
        q_three = q_chip[:, lo:hi]

        scores = jnp.einsum("qhd,khd->qhk", q_three, k_three, preferred_element_type=jnp.float32) * scale
        scores = jnp.where(keep, scores, NEG)
        best = jnp.max(scores, axis=2)
        weights = jnp.where(keep, jnp.exp(scores - best[:, :, None]), 0.0)
        total = jnp.sum(weights, axis=2)
        accum = jnp.einsum(
            "qhk,khd->qhd", weights.astype(jnp.bfloat16), v_three, preferred_element_type=jnp.float32
        )

        state = jnp.concatenate([best, total, accum.reshape(chip_rows, span * size)], axis=1)
        own_state, other_state = halves(state, core)
        got_state = swap(other_state)
        best_a, total_a, acc_a = own_state[:, :span], own_state[:, span:2 * span], own_state[:, 2 * span:]
        best_b, total_b, acc_b = got_state[:, :span], got_state[:, span:2 * span], got_state[:, 2 * span:]
        best_m = jnp.maximum(best_a, best_b)
        fa = jnp.exp(best_a - best_m)
        fb = jnp.exp(best_b - best_m)
        total_m = total_a * fa + total_b * fb
        acc_m = (
            acc_a.reshape(rows, span, size) * fa[:, :, None]
            + acc_b.reshape(rows, span, size) * fb[:, :, None]
        )
        attended_parts.append((acc_m / total_m[:, :, None]).astype(jnp.bfloat16))
        lse_parts.append(best_m + jnp.log(total_m))

    attended = jnp.concatenate(attended_parts, axis=1)

    projected = jnp.dot(attended.reshape(rows, width), out_weight, preferred_element_type=jnp.float32)
    mixed = lax.psum_scatter(projected.astype(jnp.bfloat16), "head", scatter_dimension=1, tiled=True)

    q_grads, k_grads, v_grads = [], [], []
    for (lo, hi), att, lse, (k_three, v_three) in zip(GROUPS, attended_parts, lse_parts, kv_parts):
        span = hi - lo
        q_three = q_chip[:, lo:hi]
        g_three = g_chip[:, lo:hi]
        delta = jnp.sum(g_own[:, lo:hi].astype(jnp.float32) * att.astype(jnp.float32), axis=2)
        side = jnp.concatenate([lse, delta], axis=1)
        side_chip = pair_rows(side, swap(side), core)
        lse_chip, delta_chip = side_chip[:, :span], side_chip[:, span:]

        scores = jnp.einsum("qhd,khd->qhk", q_three, k_three, preferred_element_type=jnp.float32) * scale
        probs = jnp.where(keep, jnp.exp(scores - lse_chip[:, :, None]), 0.0)
        dprob = jnp.einsum("qhd,khd->qhk", g_three, v_three, preferred_element_type=jnp.float32)
        dscore = (probs * (dprob - delta_chip[:, :, None])).astype(jnp.bfloat16)

        q_part = jnp.einsum("qhk,khd->qhd", dscore, k_three, preferred_element_type=jnp.float32) * scale
        q_own, q_other = halves(q_part.reshape(chip_rows, span * size), core)
        q_grads.append((q_own + swap(q_other)).astype(jnp.bfloat16))

        key_part = (
            jnp.einsum("qhk,qhd->khd", dscore, q_three, preferred_element_type=jnp.float32) * scale
        ).astype(jnp.bfloat16)
        value_part = jnp.einsum(
            "qhk,qhd->khd", probs.astype(jnp.bfloat16), g_three, preferred_element_type=jnp.float32
        ).astype(jnp.bfloat16)
        grad_parts = jnp.stack(
            [key_part.reshape(n_out, rows, span * size), value_part.reshape(n_out, rows, span * size)],
            axis=1,
        )
        received = lax.all_to_all(grad_parts, "ctxo", 0, 0, tiled=True)
        k_grads.append(received[:, 0])
        v_grads.append(received[:, 1])

    query_grad = jnp.concatenate(q_grads, axis=1)
    key_grad = jnp.sum(jnp.concatenate(k_grads, axis=2).astype(jnp.float32), axis=0).astype(jnp.bfloat16)
    value_grad = jnp.sum(jnp.concatenate(v_grads, axis=2).astype(jnp.float32), axis=0).astype(jnp.bfloat16)
    return (mixed, query_grad, key_grad, value_grad)


def solution(mesh):
    devices = mesh.devices
    n_ctx, n_head = devices.shape
    split = Mesh(devices.reshape(n_ctx // 2, 2, n_head), ("ctxo", "core", "head"))
    rows_spec = P(CTX, "head")
    in_specs = (rows_spec, rows_spec, rows_spec, P("head", None), rows_spec, P(), P())
    out_specs = (rows_spec, rows_spec, rows_spec, rows_spec)
    return jax.shard_map(
        per_device, mesh=split, in_specs=in_specs, out_specs=out_specs, check_vma=False
    )
```
